128 devices in a mesh: section: 4 (over x), dp: 32 (over z, y, core).
Axes of the slice: x: 4, y: 4, z: 4, core: 2. Of those that a mesh axis runs over, the one named last changes fastest.
Arguments:
- latents: bfloat16 [4, 32, 4, 16, 8, 256], P(None, 'dp'), may hold values from -36 to 36
- cotangent: bfloat16 [4, 32, 4, 16, 8, 256], P(None, 'dp'), may hold values from -6 to 6
- spatial_kernels: bfloat16 [4, 2304, 256], P('section'), may hold values from -0.125 to 0.125
- temporal_kernels: bfloat16 [4, 768, 256], P('section'), may hold values from -0.21875 to 0.21875
Outputs:
- grad_spatial: float32 [4, 2304, 256], P('section', 'dp')
- grad_temporal: float32 [4, 768, 256], P('section', 'dp')
The draws below stay inside these ranges and needn't reach their ends.
All inputs are finite; a program needn't handle non-finite values.
Results may differ from the reference program's by a relative error of at most 0.017.
Values may be sent and summed in bfloat16 or wider, within the bound.
No kernel may reach another device: no remote copies, remote signals or barrier semaphores. Data moves between devices by JAX's collectives and lax.ppermute only.
A program may use at most 128 MiB of HBM per device.

```python
import math
import jax
import jax.numpy as jnp
from jax import lax

C = 256
MICRO = 4
FR = 4
HT = 16
WD = 8
BATCH = 32
SECTIONS = 4


def draw_latents(key, part):
    shape = (MICRO, BATCH, FR, HT, WD, C)
    key_base, key_chan, key_cell = jax.random.split(key, 3)
    base = jnp.clip(jax.random.normal(key_base, shape, jnp.float32), -4.0, 4.0)
    low_end, high_end = (0.3, 3.0)
    chan_scale = jnp.exp(jax.random.uniform(key_chan, (C,), jnp.float32, math.log(low_end), math.log(high_end)))
    cell_scale = jnp.exp(jax.random.uniform(key_cell, shape[:-1] + (1,), jnp.float32, math.log(low_end), math.log(high_end)))
    return (base * chan_scale * cell_scale).astype(jnp.bfloat16)


def level_of(own_key, dims, pieces, low, top_value):
    def one(axis_at, parts):
        draws = jax.random.uniform(jax.random.fold_in(jax.random.fold_in(own_key, 6), axis_at), (parts,), jnp.float32, low / len(pieces), top_value / len(pieces))
        return jnp.repeat(jnp.exp(draws), dims[axis_at] // parts).reshape((-1,) + (1,) * (len(dims) - axis_at - 1))

    loudness = one(*pieces[0])
    for cut in pieces[1:]:
        loudness = loudness * one(*cut)
    return loudness


def centred(rng, extent, scale, limit, shards=(), held_as=jnp.bfloat16):
    entries = jax.random.normal(rng, extent, jnp.float32) * scale
    if len(shards) > 0:
        entries = level_of(rng, extent, shards, -0.22, 0.18) * entries
    return jnp.clip(entries, min=-limit, max=limit).astype(held_as)


def setup_inputs(seed: int = 0) -> dict:
    keys = jax.random.split(jax.random.key(seed), 5)
    latents = draw_latents(jax.random.fold_in(keys[4], 71), 0)
    cotangent = centred(keys[1], (MICRO, BATCH, FR, HT, WD, C), 1.0, 6.0, ((1, 32),))
    spatial_kernels = centred(keys[2], (SECTIONS, 9 * C, C), (9 * C) ** -0.5, 0.125, ((0, 4),))
    temporal_kernels = centred(keys[3], (SECTIONS, 3 * C, C), (3 * C) ** -0.5, 0.21875, ((0, 4),))
    return {"latents": latents, "cotangent": cotangent, "spatial_kernels": spatial_kernels, "temporal_kernels": temporal_kernels}


def silu_slope(value):
    sig = jax.nn.sigmoid(value)
    return sig * (1.0 + value * (1.0 - sig))

def flatten_cells(array):
    return array.reshape(-1, array.shape[-1])

def spatial_cols(source):
    height, width = (source.shape[2], source.shape[3])
    padded = jnp.pad(source, ((0, 0), (0, 0), (1, 1), (1, 1), (0, 0)))
    return jnp.concatenate([padded[:, :, row_tap:row_tap + height, col_tap:col_tap + width, :] for row_tap in range(3) for col_tap in range(3)], axis=-1)

def temporal_cols(source):
    frames = source.shape[1]
    padded = jnp.pad(source, ((0, 0), (2, 0), (0, 0), (0, 0), (0, 0)))
    return jnp.concatenate([padded[:, tap:tap + frames] for tap in range(3)], axis=-1)

def spatial_fold(columns, channels):
    height, width = (columns.shape[2], columns.shape[3])
    padded = jnp.pad(columns, ((0, 0), (0, 0), (1, 1), (1, 1), (0, 0)))
    total = jnp.zeros(columns.shape[:-1] + (channels,), jnp.float32)
    for row_tap in range(3):
        for col_tap in range(3):
            tap = row_tap * 3 + col_tap
            total = total + padded[:, :, 2 - row_tap:2 - row_tap + height, 2 - col_tap:2 - col_tap + width, tap * channels:(tap + 1) * channels]
    return total

def temporal_fold(columns, channels):
    frames = columns.shape[1]
    padded = jnp.pad(columns, ((0, 0), (0, 2), (0, 0), (0, 0), (0, 0)))
    total = jnp.zeros(columns.shape[:-1] + (channels,), jnp.float32)
    for tap in range(3):
        total = total + padded[:, 2 - tap:2 - tap + frames, :, :, tap * channels:(tap + 1) * channels]
    return total

def section_forward(section_in, w_spatial, w_temporal):
    act_f32 = section_in.astype(jnp.float32)
    inv_rms = lax.rsqrt(lax.optimization_barrier(jnp.mean(act_f32 * act_f32, axis=-1, keepdims=True)) + 1e-06)
    silu_one = jax.nn.silu(act_f32 * inv_rms).astype(jnp.bfloat16)
    cols_space = spatial_cols(silu_one)
    middle = jnp.dot(flatten_cells(cols_space), w_spatial, preferred_element_type=jnp.float32).reshape(section_in.shape)
    silu_two = jax.nn.silu(middle).astype(jnp.bfloat16)
    cols_time = temporal_cols(silu_two)
    branch = jnp.dot(flatten_cells(cols_time), w_temporal, preferred_element_type=jnp.float32).reshape(section_in.shape)
    return ((act_f32 + branch).astype(jnp.bfloat16), middle)

def section_backward(grad_out, section_in, middle, w_spatial, w_temporal):
    channels = section_in.shape[-1]
    act_f32 = section_in.astype(jnp.float32)
    inv_rms = lax.rsqrt(lax.optimization_barrier(jnp.mean(act_f32 * act_f32, axis=-1, keepdims=True)) + 1e-06)
    normed = act_f32 * inv_rms
    cols_space = spatial_cols(jax.nn.silu(normed).astype(jnp.bfloat16))
    cols_time = temporal_cols(jax.nn.silu(middle).astype(jnp.bfloat16))
    back_time = lax.dot_general(flatten_cells(grad_out), w_temporal, (((1,), (1,)), ((), ())), preferred_element_type=jnp.float32)
    time_back = temporal_fold(back_time.reshape(section_in.shape[:-1] + (3 * channels,)), channels)
    grad_mid = (time_back * silu_slope(middle)).astype(jnp.bfloat16)
    back_space = lax.dot_general(flatten_cells(grad_mid), w_spatial, (((1,), (1,)), ((), ())), preferred_element_type=jnp.float32)
    space_back = spatial_fold(back_space.reshape(section_in.shape[:-1] + (9 * channels,)), channels)
    grad_norm = space_back * silu_slope(normed)
    grad_act = inv_rms * grad_norm - act_f32 * (inv_rms * inv_rms * inv_rms) * lax.optimization_barrier(jnp.mean(grad_norm * act_f32, axis=-1, keepdims=True))
    grad_in = (grad_out.astype(jnp.float32) + grad_act).astype(jnp.bfloat16)
    return (cols_space, grad_mid, cols_time, grad_in)

def kernel_term(columns, grads):
    return lax.dot_general(flatten_cells(columns), flatten_cells(grads), (((0,), (0,)), ((), ())), preferred_element_type=jnp.float32)

def reference(latents, cotangent, spatial_kernels, temporal_kernels):
    section_count = spatial_kernels.shape[0]
    micro_count = latents.shape[0]
    sums_space = [jnp.zeros(spatial_kernels.shape[1:], jnp.float32) for _ in range(section_count)]
    sums_time = [jnp.zeros(temporal_kernels.shape[1:], jnp.float32) for _ in range(section_count)]
    for micro_idx in range(micro_count):
        current = latents[micro_idx]
        inputs = []
        middles = []
        for section_idx in range(section_count):
            inputs.append(current)
            current, middle = section_forward(current, spatial_kernels[section_idx], temporal_kernels[section_idx])
            middles.append(middle)
        grad_now = cotangent[micro_idx]
        for section_idx in range(section_count - 1, -1, -1):
            cols_space, grad_mid, cols_time, grad_in = section_backward(grad_now, inputs[section_idx], middles[section_idx], spatial_kernels[section_idx], temporal_kernels[section_idx])
            sums_space[section_idx] = sums_space[section_idx] + kernel_term(cols_space, grad_mid)
            sums_time[section_idx] = sums_time[section_idx] + kernel_term(cols_time, grad_now)
            grad_now = grad_in
    cells = latents.shape[0] * latents.shape[1] * latents.shape[2] * latents.shape[3] * latents.shape[4]
    grad_scale = 1.0 / math.sqrt(cells)
    return (grad_scale * jnp.stack(sums_space), grad_scale * jnp.stack(sums_time))
```

```python
import math

import jax
import jax.numpy as jnp
from jax import lax
from jax.sharding import PartitionSpec as P


def from_behind(value, axis, steps):
    count = lax.axis_size(axis)
    first, last = (max(0, -steps), min(count, count - steps))
    return lax.ppermute(value, axis, [(source, source + steps) for source in range(first, last)])


def silu_slope(value):
    sig = jax.nn.sigmoid(value)
    return sig * (1.0 + value * (1.0 - sig))


def flatten_cells(array):
    return array.reshape(-1, array.shape[-1])


def spatial_cols(source):
    height, width = (source.shape[2], source.shape[3])
    padded = jnp.pad(source, ((0, 0), (0, 0), (1, 1), (1, 1), (0, 0)))
    return jnp.concatenate(
        [
            padded[:, :, row_tap : row_tap + height, col_tap : col_tap + width, :]
            for row_tap in range(3)
            for col_tap in range(3)
        ],
        axis=-1,
    )


def temporal_cols(source):
    frames = source.shape[1]
    padded = jnp.pad(source, ((0, 0), (2, 0), (0, 0), (0, 0), (0, 0)))
    return jnp.concatenate([padded[:, tap : tap + frames] for tap in range(3)], axis=-1)


def spatial_fold(columns, channels):
    height, width = (columns.shape[2], columns.shape[3])
    padded = jnp.pad(columns, ((0, 0), (0, 0), (1, 1), (1, 1), (0, 0)))
    total = jnp.zeros(columns.shape[:-1] + (channels,), jnp.float32)
    for row_tap in range(3):
        for col_tap in range(3):
            tap = row_tap * 3 + col_tap
            total = (
                total
                + padded[
                    :,
                    :,
                    2 - row_tap : 2 - row_tap + height,
                    2 - col_tap : 2 - col_tap + width,
                    tap * channels : (tap + 1) * channels,
                ]
            )
    return total


def temporal_fold(columns, channels):
    frames = columns.shape[1]
    padded = jnp.pad(columns, ((0, 0), (0, 2), (0, 0), (0, 0), (0, 0)))
    total = jnp.zeros(columns.shape[:-1] + (channels,), jnp.float32)
    for tap in range(3):
        total = (
            total
            + padded[:, 2 - tap : 2 - tap + frames, :, :, tap * channels : (tap + 1) * channels]
        )
    return total


def section_forward(section_in, w_spatial, w_temporal):
    act_f32 = section_in.astype(jnp.float32)
    inv_rms = lax.rsqrt(jnp.mean(act_f32 * act_f32, axis=-1, keepdims=True) + 1e-06)
    silu_one = jax.nn.silu(act_f32 * inv_rms).astype(jnp.bfloat16)
    cols_space = spatial_cols(silu_one)
    middle = jnp.dot(
        flatten_cells(cols_space), w_spatial, preferred_element_type=jnp.float32
    ).reshape(section_in.shape)
    silu_two = jax.nn.silu(middle).astype(jnp.bfloat16)
    cols_time = temporal_cols(silu_two)
    branch = jnp.dot(
        flatten_cells(cols_time), w_temporal, preferred_element_type=jnp.float32
    ).reshape(section_in.shape)
    return ((act_f32 + branch).astype(jnp.bfloat16), middle)


def section_backward(grad_out, section_in, middle, w_spatial, w_temporal):
    channels = section_in.shape[-1]
    act_f32 = section_in.astype(jnp.float32)
    inv_rms = lax.rsqrt(jnp.mean(act_f32 * act_f32, axis=-1, keepdims=True) + 1e-06)
    normed = act_f32 * inv_rms
    cols_space = spatial_cols(jax.nn.silu(normed).astype(jnp.bfloat16))
    cols_time = temporal_cols(jax.nn.silu(middle).astype(jnp.bfloat16))
    back_time = lax.dot_general(
        flatten_cells(grad_out),
        w_temporal,
        (((1,), (1,)), ((), ())),
        preferred_element_type=jnp.float32,
    )
    time_back = temporal_fold(back_time.reshape(section_in.shape[:-1] + (3 * channels,)), channels)
    grad_mid = (time_back * silu_slope(middle)).astype(jnp.bfloat16)
    back_space = lax.dot_general(
        flatten_cells(grad_mid),
        w_spatial,
        (((1,), (1,)), ((), ())),
        preferred_element_type=jnp.float32,
    )
    space_back = spatial_fold(back_space.reshape(section_in.shape[:-1] + (9 * channels,)), channels)
    grad_norm = space_back * silu_slope(normed)
    grad_act = inv_rms * grad_norm - act_f32 * (inv_rms * inv_rms * inv_rms) * jnp.mean(
        grad_norm * act_f32, axis=-1, keepdims=True
    )
    grad_in = (grad_out.astype(jnp.float32) + grad_act).astype(jnp.bfloat16)
    return (cols_space, grad_mid, cols_time, grad_in)


def kernel_term(columns, grads):
    return lax.dot_general(
        flatten_cells(columns),
        flatten_cells(grads),
        (((0,), (0,)), ((), ())),
        preferred_element_type=jnp.float32,
    )


def store_slot(stash, slot_idx, active, value):
    before = lax.dynamic_index_in_dim(stash, slot_idx, 0, keepdims=False)
    return lax.dynamic_update_index_in_dim(stash, jnp.where(active, value, before), slot_idx, 0)


def local(latents, cotangent, spatial_kernels, temporal_kernels):
    w_spatial = spatial_kernels[0]
    w_temporal = temporal_kernels[0]
    micro_count = latents.shape[0]
    section_count = lax.axis_size("section")
    replicas = lax.axis_size("dp")
    tick_count = micro_count + section_count - 1
    section_idx = lax.axis_index("section")
    is_first = section_idx == 0
    is_last = section_idx == section_count - 1
    empty_act = jnp.zeros(latents.shape[1:], jnp.bfloat16)
    stash_in = jnp.zeros(latents.shape, jnp.bfloat16)
    stash_mid = jnp.zeros(latents.shape, jnp.float32)
    received = empty_act
    for step_idx in range(tick_count):
        fresh_in = latents[step_idx] if step_idx < micro_count else empty_act
        section_in = jnp.where(is_first, fresh_in, received)
        section_out, middle = section_forward(section_in, w_spatial, w_temporal)
        micro_idx = step_idx - section_idx
        active = (micro_idx >= 0) & (micro_idx < micro_count)
        slot_idx = jnp.clip(micro_idx, 0, micro_count - 1)
        stash_in = store_slot(stash_in, slot_idx, active, section_in)
        stash_mid = store_slot(stash_mid, slot_idx, active, middle)
        if step_idx < tick_count - 1:
            received = from_behind(section_out, "section", 1)
    hold_space = jnp.zeros(w_spatial.shape, jnp.float32)
    hold_time = jnp.zeros(w_temporal.shape, jnp.float32)
    received = empty_act
    for step_idx in range(tick_count):
        fresh_grad = cotangent[step_idx] if step_idx < micro_count else empty_act
        grad_now = jnp.where(is_last, fresh_grad, received)
        micro_idx = step_idx - (section_count - 1 - section_idx)
        active = (micro_idx >= 0) & (micro_idx < micro_count)
        slot_idx = jnp.clip(micro_idx, 0, micro_count - 1)
        section_in = lax.dynamic_index_in_dim(stash_in, slot_idx, 0, keepdims=False)
        middle = lax.dynamic_index_in_dim(stash_mid, slot_idx, 0, keepdims=False)
        cols_space, grad_mid, cols_time, grad_in = section_backward(
            grad_now, section_in, middle, w_spatial, w_temporal
        )
        active_weight = active.astype(jnp.float32)
        hold_space = hold_space + active_weight * kernel_term(cols_space, grad_mid)
        hold_time = hold_time + active_weight * kernel_term(cols_time, grad_now)
        if step_idx < tick_count - 1:
            received = from_behind(grad_in, "section", -1)
    rows_space = w_spatial.shape[0] // replicas
    rows_time = w_temporal.shape[0] // replicas
    packed = jnp.concatenate(
        [
            hold_space.reshape(replicas, rows_space, -1),
            hold_time.reshape(replicas, rows_time, -1),
        ],
        axis=1,
    ).astype(jnp.bfloat16)
    gathered = lax.all_to_all(packed, "dp", 0, 0, tiled=True)
    share = jnp.sum(gathered.astype(jnp.float32), axis=0)
    share_space, share_time = (share[:rows_space], share[rows_space:])
    cells = (
        micro_count
        * replicas
        * latents.shape[1]
        * latents.shape[2]
        * latents.shape[3]
        * latents.shape[4]
    )
    grad_scale = 1.0 / math.sqrt(cells)
    return ((grad_scale * share_space)[None], (grad_scale * share_time)[None])


def solution(mesh):
    in_specs = (
        P(None, "dp", None, None, None, None),
        P(None, "dp", None, None, None, None),
        P("section", None, None),
        P("section", None, None),
    )
    out_specs = (P("section", "dp", None), P("section", "dp", None))
    return jax.shard_map(local, mesh=mesh, in_specs=in_specs, out_specs=out_specs, check_vma=False)
```

```python
import math

import jax
import jax.numpy as jnp
from jax import lax
import numpy as np
from jax.sharding import Mesh, PartitionSpec as P


def from_behind(value, axis, steps):
    count = lax.axis_size(axis)
    first, last = (max(0, -steps), min(count, count - steps))
    return lax.ppermute(value, axis, [(source, source + steps) for source in range(first, last)])


def silu_slope(value):
    sig = jax.nn.sigmoid(value)
    return sig * (1.0 + value * (1.0 - sig))


def flatten_cells(array):
    return array.reshape(-1, array.shape[-1])


def spatial_cols(source):
    height, width = (source.shape[2], source.shape[3])
    padded = jnp.pad(source, ((0, 0), (0, 0), (1, 1), (1, 1), (0, 0)))
    return jnp.concatenate(
        [
            padded[:, :, row_tap : row_tap + height, col_tap : col_tap + width, :]
            for row_tap in range(3)
            for col_tap in range(3)
        ],
        axis=-1,
    )


def temporal_cols(source):
    frames = source.shape[1]
    padded = jnp.pad(source, ((0, 0), (2, 0), (0, 0), (0, 0), (0, 0)))
    return jnp.concatenate([padded[:, tap : tap + frames] for tap in range(3)], axis=-1)


def spatial_fold(columns, channels):
    height, width = (columns.shape[2], columns.shape[3])
    padded = jnp.pad(columns, ((0, 0), (0, 0), (1, 1), (1, 1), (0, 0)))
    total = jnp.zeros(columns.shape[:-1] + (channels,), jnp.float32)
    for row_tap in range(3):
        for col_tap in range(3):
            tap = row_tap * 3 + col_tap
            total = (
                total
                + padded[
                    :,
                    :,
                    2 - row_tap : 2 - row_tap + height,
                    2 - col_tap : 2 - col_tap + width,
                    tap * channels : (tap + 1) * channels,
                ]
            )
    return total


def temporal_fold(columns, channels):
    frames = columns.shape[1]
    padded = jnp.pad(columns, ((0, 0), (0, 2), (0, 0), (0, 0), (0, 0)))
    total = jnp.zeros(columns.shape[:-1] + (channels,), jnp.float32)
    for tap in range(3):
        total = (
            total
            + padded[:, 2 - tap : 2 - tap + frames, :, :, tap * channels : (tap + 1) * channels]
        )
    return total


def section_forward(section_in, w_spatial, w_temporal):
    act_f32 = section_in.astype(jnp.float32)
    inv_rms = lax.rsqrt(jnp.mean(act_f32 * act_f32, axis=-1, keepdims=True) + 1e-06)
    silu_one = jax.nn.silu(act_f32 * inv_rms).astype(jnp.bfloat16)
    cols_space = spatial_cols(silu_one)
    middle = jnp.dot(
        flatten_cells(cols_space), w_spatial, preferred_element_type=jnp.float32
    ).reshape(section_in.shape)
    silu_two = jax.nn.silu(middle).astype(jnp.bfloat16)
    cols_time = temporal_cols(silu_two)
    branch = jnp.dot(
        flatten_cells(cols_time), w_temporal, preferred_element_type=jnp.float32
    ).reshape(section_in.shape)
    return ((act_f32 + branch).astype(jnp.bfloat16), middle)


def section_backward(grad_out, section_in, middle, w_spatial, w_temporal):
    channels = section_in.shape[-1]
    act_f32 = section_in.astype(jnp.float32)
    inv_rms = lax.rsqrt(jnp.mean(act_f32 * act_f32, axis=-1, keepdims=True) + 1e-06)
    normed = act_f32 * inv_rms
    cols_space = spatial_cols(jax.nn.silu(normed).astype(jnp.bfloat16))
    cols_time = temporal_cols(jax.nn.silu(middle).astype(jnp.bfloat16))
    back_time = lax.dot_general(
        flatten_cells(grad_out),
        w_temporal,
        (((1,), (1,)), ((), ())),
        preferred_element_type=jnp.float32,
    )
    time_back = temporal_fold(back_time.reshape(section_in.shape[:-1] + (3 * channels,)), channels)
    grad_mid = (time_back * silu_slope(middle)).astype(jnp.bfloat16)
    back_space = lax.dot_general(
        flatten_cells(grad_mid),
        w_spatial,
        (((1,), (1,)), ((), ())),
        preferred_element_type=jnp.float32,
    )
    space_back = spatial_fold(back_space.reshape(section_in.shape[:-1] + (9 * channels,)), channels)
    grad_norm = space_back * silu_slope(normed)
    grad_act = inv_rms * grad_norm - act_f32 * (inv_rms * inv_rms * inv_rms) * jnp.mean(
        grad_norm * act_f32, axis=-1, keepdims=True
    )
    grad_in = (grad_out.astype(jnp.float32) + grad_act).astype(jnp.bfloat16)
    return (cols_space, grad_mid, cols_time, grad_in)


def kernel_term(columns, grads):
    return lax.dot_general(
        flatten_cells(columns),
        flatten_cells(grads),
        (((0,), (0,)), ((), ())),
        preferred_element_type=jnp.float32,
    )


def pick_by_section(section_idx, candidates):
    chosen = candidates[0]
    for idx in range(1, len(candidates)):
        chosen = jnp.where(section_idx == idx, candidates[idx], chosen)
    return chosen


def reduce_over_dp(packed):
    cores = lax.axis_size("core")
    core_idx = lax.axis_index("core")
    by_core = packed.reshape(-1, cores, *packed.shape[1:])
    keep = lax.dynamic_index_in_dim(by_core, core_idx, 1, keepdims=False)
    send = lax.dynamic_index_in_dim(by_core, cores - 1 - core_idx, 1, keepdims=False)
    got = lax.ppermute(send.astype(jnp.bfloat16), "core", [(0, 1), (1, 0)])
    pair_sum = (keep + got.astype(jnp.float32)).astype(jnp.bfloat16)
    gathered = lax.all_to_all(pair_sum, "chip", 0, 0, tiled=True)
    return jnp.sum(gathered.astype(jnp.float32), axis=0)


def local(latents, cotangent, spatial_kernels, temporal_kernels):
    w_spatial = spatial_kernels[0]
    w_temporal = temporal_kernels[0]
    micro_count = latents.shape[0]
    section_count = lax.axis_size("section")
    replicas = lax.axis_size("chip") * lax.axis_size("core")
    section_idx = lax.axis_index("section")
    is_first = section_idx == 0
    is_last = section_idx == section_count - 1
    fwd_last = micro_count + section_count - 2
    bwd_first = section_count - 1
    tick_count = micro_count + 2 * section_count - 2
    empty_act = jnp.zeros(latents.shape[1:], jnp.bfloat16)
    empty_mid = jnp.zeros(latents.shape[1:], jnp.float32)
    stash_in = []
    stash_mid = []
    hold_space = jnp.zeros(w_spatial.shape, jnp.float32)
    hold_time = jnp.zeros(w_temporal.shape, jnp.float32)
    recv_act = empty_act
    recv_grad = empty_act
    for tick in range(tick_count):
        if tick <= fwd_last:
            fresh_in = latents[tick] if tick < micro_count else empty_act
            section_in = jnp.where(is_first, fresh_in, recv_act)
            section_out, middle = section_forward(section_in, w_spatial, w_temporal)
            stash_in.append(section_in)
            stash_mid.append(middle)
        if tick >= bwd_first:
            fresh_idx = tick - bwd_first
            fresh_grad = cotangent[fresh_idx] if fresh_idx < micro_count else empty_act
            grad_now = jnp.where(is_last, fresh_grad, recv_grad)
            micro_idx = tick - 2 * (section_count - 1) + section_idx
            active = (micro_idx >= 0) & (micro_idx < micro_count)
            cand_in = []
            cand_mid = []
            for sec in range(section_count):
                fwd_tick = tick - 2 * (section_count - 1) + 2 * sec
                fwd_micro = fwd_tick - sec
                if 0 <= fwd_micro < micro_count:
                    cand_in.append(stash_in[fwd_tick])
                    cand_mid.append(stash_mid[fwd_tick])
                else:
                    cand_in.append(empty_act)
                    cand_mid.append(empty_mid)
            section_in_b = pick_by_section(section_idx, cand_in)
            middle_b = pick_by_section(section_idx, cand_mid)
            cols_space, grad_mid, cols_time, grad_in = section_backward(
                grad_now, section_in_b, middle_b, w_spatial, w_temporal
            )
            active_weight = active.astype(jnp.float32)
            hold_space = hold_space + active_weight * kernel_term(cols_space, grad_mid)
            hold_time = hold_time + active_weight * kernel_term(cols_time, grad_now)
        if tick + 1 <= fwd_last:
            recv_act = from_behind(section_out, "section", 1)
        if tick >= bwd_first and tick + 1 < tick_count:
            recv_grad = from_behind(grad_in, "section", -1)
    rows_space = w_spatial.shape[0] // replicas
    rows_time = w_temporal.shape[0] // replicas
    packed = jnp.concatenate(
        [
            hold_space.reshape(replicas, rows_space, -1),
            hold_time.reshape(replicas, rows_time, -1),
        ],
        axis=1,
    )
    share = reduce_over_dp(packed)
    share_space, share_time = (share[:rows_space], share[rows_space:])
    cells = (
        micro_count
        * replicas
        * latents.shape[1]
        * latents.shape[2]
        * latents.shape[3]
        * latents.shape[4]
    )
    grad_scale = 1.0 / math.sqrt(cells)
    return ((grad_scale * share_space)[None], (grad_scale * share_time)[None])


def solution(mesh):
    cores = 2
    chip_mesh = Mesh(
        np.asarray(mesh.devices).reshape(mesh.shape["section"], mesh.shape["dp"] // cores, cores),
        ("section", "chip", "core"),
    )
    dp = ("chip", "core")
    in_specs = (
        P(None, dp, None, None, None, None),
        P(None, dp, None, None, None, None),
        P("section", None, None),
        P("section", None, None),
    )
    out_specs = (P("section", dp, None), P("section", dp, None))
    return jax.shard_map(local, mesh=chip_mesh, in_specs=in_specs, out_specs=out_specs, check_vma=False)
```

```python
import math

import jax
import jax.numpy as jnp
from jax import lax
import numpy as np
from jax.sharding import Mesh, PartitionSpec as P


def from_behind(value, axis, steps):
    count = lax.axis_size(axis)
    first, last = (max(0, -steps), min(count, count - steps))
    return lax.ppermute(value, axis, [(source, source + steps) for source in range(first, last)])


def silu_slope(value):
    sig = jax.nn.sigmoid(value)
    return sig * (1.0 + value * (1.0 - sig))


def flatten_cells(array):
    return array.reshape(-1, array.shape[-1])


def spatial_cols(source):
    height, width = (source.shape[2], source.shape[3])
    padded = jnp.pad(source, ((0, 0), (0, 0), (1, 1), (1, 1), (0, 0)))
    return jnp.concatenate(
        [
            padded[:, :, row_tap : row_tap + height, col_tap : col_tap + width, :]
            for row_tap in range(3)
            for col_tap in range(3)
        ],
        axis=-1,
    )


def temporal_cols(source):
    frames = source.shape[1]
    padded = jnp.pad(source, ((0, 0), (2, 0), (0, 0), (0, 0), (0, 0)))
    return jnp.concatenate([padded[:, tap : tap + frames] for tap in range(3)], axis=-1)


def spatial_fold(columns, channels):
    height, width = (columns.shape[2], columns.shape[3])
    padded = jnp.pad(columns, ((0, 0), (0, 0), (1, 1), (1, 1), (0, 0)))
    total = jnp.zeros(columns.shape[:-1] + (channels,), jnp.float32)
    for row_tap in range(3):
        for col_tap in range(3):
            tap = row_tap * 3 + col_tap
            total = (
                total
                + padded[
                    :,
                    :,
                    2 - row_tap : 2 - row_tap + height,
                    2 - col_tap : 2 - col_tap + width,
                    tap * channels : (tap + 1) * channels,
                ]
            )
    return total


def temporal_fold(columns, channels):
    frames = columns.shape[1]
    padded = jnp.pad(columns, ((0, 0), (0, 2), (0, 0), (0, 0), (0, 0)))
    total = jnp.zeros(columns.shape[:-1] + (channels,), jnp.float32)
    for tap in range(3):
        total = (
            total
            + padded[:, 2 - tap : 2 - tap + frames, :, :, tap * channels : (tap + 1) * channels]
        )
    return total


def section_forward(section_in, w_spatial, w_temporal):
    act_f32 = section_in.astype(jnp.float32)
    inv_rms = lax.rsqrt(jnp.mean(act_f32 * act_f32, axis=-1, keepdims=True) + 1e-06)
    silu_one = jax.nn.silu(act_f32 * inv_rms).astype(jnp.bfloat16)
    cols_space = spatial_cols(silu_one)
    middle = jnp.dot(
        flatten_cells(cols_space), w_spatial, preferred_element_type=jnp.float32
    ).reshape(section_in.shape)
    silu_two = jax.nn.silu(middle).astype(jnp.bfloat16)
    cols_time = temporal_cols(silu_two)
    branch = jnp.dot(
        flatten_cells(cols_time), w_temporal, preferred_element_type=jnp.float32
    ).reshape(section_in.shape)
    return ((act_f32 + branch).astype(jnp.bfloat16), middle)


def section_recompute(section_in, w_spatial):
    act_f32 = section_in.astype(jnp.float32)
    inv_rms = lax.rsqrt(jnp.mean(act_f32 * act_f32, axis=-1, keepdims=True) + 1e-06)
    normed = act_f32 * inv_rms
    cols_space = spatial_cols(jax.nn.silu(normed).astype(jnp.bfloat16))
    middle = jnp.dot(
        flatten_cells(cols_space), w_spatial, preferred_element_type=jnp.float32
    ).reshape(section_in.shape)
    return act_f32, inv_rms, normed, cols_space, middle


def section_backward(grad_out, act_f32, inv_rms, normed, middle, w_spatial, w_temporal):
    channels = act_f32.shape[-1]
    cols_time = temporal_cols(jax.nn.silu(middle).astype(jnp.bfloat16))
    back_time = lax.dot_general(
        flatten_cells(grad_out),
        w_temporal,
        (((1,), (1,)), ((), ())),
        preferred_element_type=jnp.float32,
    )
    time_back = temporal_fold(back_time.reshape(act_f32.shape[:-1] + (3 * channels,)), channels)
    grad_mid = (time_back * silu_slope(middle)).astype(jnp.bfloat16)
    back_space = lax.dot_general(
        flatten_cells(grad_mid),
        w_spatial,
        (((1,), (1,)), ((), ())),
        preferred_element_type=jnp.float32,
    )
    space_back = spatial_fold(back_space.reshape(act_f32.shape[:-1] + (9 * channels,)), channels)
    grad_norm = space_back * silu_slope(normed)
    grad_act = inv_rms * grad_norm - act_f32 * (inv_rms * inv_rms * inv_rms) * jnp.mean(
        grad_norm * act_f32, axis=-1, keepdims=True
    )
    grad_in = (grad_out.astype(jnp.float32) + grad_act).astype(jnp.bfloat16)
    return (grad_mid, cols_time, grad_in)


def kernel_term(columns, grads):
    return lax.dot_general(
        flatten_cells(columns),
        flatten_cells(grads),
        (((0,), (0,)), ((), ())),
        preferred_element_type=jnp.float32,
    )


def reduce_over_dp(packed):
    cores = lax.axis_size("core")
    core_idx = lax.axis_index("core")
    by_core = packed.reshape(-1, cores, *packed.shape[1:])
    keep = lax.dynamic_index_in_dim(by_core, core_idx, 1, keepdims=False)
    send = lax.dynamic_index_in_dim(by_core, cores - 1 - core_idx, 1, keepdims=False)
    got = lax.ppermute(send.astype(jnp.bfloat16), "core", [(0, 1), (1, 0)])
    pair_sum = (keep + got.astype(jnp.float32)).astype(jnp.bfloat16)
    gathered = lax.all_to_all(pair_sum, "chip", 0, 0, tiled=True)
    return jnp.sum(gathered.astype(jnp.float32), axis=0)


def local(latents, cotangent, spatial_kernels, temporal_kernels):
    w_spatial = spatial_kernels[0]
    w_temporal = temporal_kernels[0]
    micro_count = latents.shape[0]
    section_count = lax.axis_size("section")
    replicas = lax.axis_size("chip") * lax.axis_size("core")
    section_idx = lax.axis_index("section")
    is_first = section_idx == 0
    is_last = section_idx == section_count - 1
    fwd_last = micro_count + section_count - 2
    bwd_first = section_count - 1
    tick_count = micro_count + 2 * section_count - 2
    empty_act = jnp.zeros(latents.shape[1:], jnp.bfloat16)
    stash_in = jnp.zeros((fwd_last + 1,) + latents.shape[1:], jnp.bfloat16)
    hold_space = jnp.zeros(w_spatial.shape, jnp.float32)
    hold_time = jnp.zeros(w_temporal.shape, jnp.float32)
    recv_act = empty_act
    grad_in = None
    for tick in range(tick_count):
        if grad_in is not None:
            recv_grad = from_behind(grad_in, "section", -1)
        if tick <= fwd_last:
            fresh_in = latents[tick] if tick < micro_count else empty_act
            section_in = jnp.where(is_first, fresh_in, recv_act)
            section_out, _ = section_forward(section_in, w_spatial, w_temporal)
            stash_in = stash_in.at[tick].set(section_in)
            if tick + 1 <= fwd_last:
                recv_act = from_behind(section_out, "section", 1)
        if tick >= bwd_first:
            fresh_idx = tick - bwd_first
            fresh_grad = cotangent[fresh_idx] if fresh_idx < micro_count else empty_act
            grad_now = jnp.where(is_last, fresh_grad, recv_grad) if tick > bwd_first else fresh_grad
            micro_idx = tick - 2 * (section_count - 1) + section_idx
            active = (micro_idx >= 0) & (micro_idx < micro_count)
            slot_idx = jnp.clip(micro_idx + section_idx, 0, fwd_last)
            section_in_b = lax.dynamic_index_in_dim(stash_in, slot_idx, 0, keepdims=False)
            act_f32, inv_rms, normed, cols_space, middle_b = section_recompute(
                section_in_b, w_spatial
            )
            grad_mid, cols_time, grad_in = section_backward(
                grad_now, act_f32, inv_rms, normed, middle_b, w_spatial, w_temporal
            )
            active_weight = active.astype(jnp.float32)
            hold_space = lax.optimization_barrier(
                hold_space + active_weight * kernel_term(cols_space, grad_mid)
            )
            hold_time = lax.optimization_barrier(
                hold_time + active_weight * kernel_term(cols_time, grad_now)
            )
            if tick + 1 >= tick_count:
                grad_in = None
    rows_space = w_spatial.shape[0] // replicas
    rows_time = w_temporal.shape[0] // replicas
    packed = jnp.concatenate(
        [
            hold_space.reshape(replicas, rows_space, -1),
            hold_time.reshape(replicas, rows_time, -1),
        ],
        axis=1,
    )
    share = reduce_over_dp(packed)
    share_space, share_time = (share[:rows_space], share[rows_space:])
    cells = (
        micro_count
        * replicas
        * latents.shape[1]
        * latents.shape[2]
        * latents.shape[3]
        * latents.shape[4]
    )
    grad_scale = 1.0 / math.sqrt(cells)
    return ((grad_scale * share_space)[None], (grad_scale * share_time)[None])


def solution(mesh):
    cores = 2
    chip_mesh = Mesh(
        np.asarray(mesh.devices).reshape(mesh.shape["section"], mesh.shape["dp"] // cores, cores),
        ("section", "chip", "core"),
    )
    dp = ("chip", "core")
    in_specs = (
        P(None, dp, None, None, None, None),
        P(None, dp, None, None, None, None),
        P("section", None, None),
        P("section", None, None),
    )
    out_specs = (P("section", dp, None), P("section", dp, None))
    return jax.shard_map(local, mesh=chip_mesh, in_specs=in_specs, out_specs=out_specs, check_vma=False)
```

```python
import math

import jax
import jax.numpy as jnp
from jax import lax
import numpy as np
from jax.sharding import Mesh, PartitionSpec as P


def from_behind(value, axis, steps):
    count = lax.axis_size(axis)
    first, last = (max(0, -steps), min(count, count - steps))
    return lax.ppermute(value, axis, [(source, source + steps) for source in range(first, last)])


def silu_slope(value):
    sig = jax.nn.sigmoid(value)
    return sig * (1.0 + value * (1.0 - sig))


def flatten_cells(array):
    return array.reshape(-1, array.shape[-1])


def spatial_cols(source):
    height, width = (source.shape[2], source.shape[3])
    padded = jnp.pad(source, ((0, 0), (0, 0), (1, 1), (1, 1), (0, 0)))
    return jnp.concatenate(
        [
            padded[:, :, row_tap : row_tap + height, col_tap : col_tap + width, :]
            for row_tap in range(3)
            for col_tap in range(3)
        ],
        axis=-1,
    )


def temporal_cols(source):
    frames = source.shape[1]
    padded = jnp.pad(source, ((0, 0), (2, 0), (0, 0), (0, 0), (0, 0)))
    return jnp.concatenate([padded[:, tap : tap + frames] for tap in range(3)], axis=-1)


def spatial_fold(columns, channels):
    height, width = (columns.shape[2], columns.shape[3])
    padded = jnp.pad(columns, ((0, 0), (0, 0), (1, 1), (1, 1), (0, 0)))
    total = jnp.zeros(columns.shape[:-1] + (channels,), jnp.float32)
    for row_tap in range(3):
        for col_tap in range(3):
            tap = row_tap * 3 + col_tap
            total = (
                total
                + padded[
                    :,
                    :,
                    2 - row_tap : 2 - row_tap + height,
                    2 - col_tap : 2 - col_tap + width,
                    tap * channels : (tap + 1) * channels,
                ]
            )
    return total


def temporal_fold(columns, channels):
    frames = columns.shape[1]
    padded = jnp.pad(columns, ((0, 0), (0, 2), (0, 0), (0, 0), (0, 0)))
    total = jnp.zeros(columns.shape[:-1] + (channels,), jnp.float32)
    for tap in range(3):
        total = (
            total
            + padded[:, 2 - tap : 2 - tap + frames, :, :, tap * channels : (tap + 1) * channels]
        )
    return total


def section_forward(section_in, w_spatial, w_temporal):
    act_f32 = section_in.astype(jnp.float32)
    inv_rms = lax.rsqrt(jnp.mean(act_f32 * act_f32, axis=-1, keepdims=True) + 1e-06)
    silu_one = jax.nn.silu(act_f32 * inv_rms).astype(jnp.bfloat16)
    cols_space = spatial_cols(silu_one)
    middle = jnp.dot(
        flatten_cells(cols_space), w_spatial, preferred_element_type=jnp.float32
    ).reshape(section_in.shape)
    silu_two = jax.nn.silu(middle).astype(jnp.bfloat16)
    cols_time = temporal_cols(silu_two)
    branch = jnp.dot(
        flatten_cells(cols_time), w_temporal, preferred_element_type=jnp.float32
    ).reshape(section_in.shape)
    return ((act_f32 + branch).astype(jnp.bfloat16), middle)


def section_backward(grad_out, section_in, middle, w_spatial, w_temporal):
    channels = section_in.shape[-1]
    act_f32 = section_in.astype(jnp.float32)
    inv_rms = lax.rsqrt(jnp.mean(act_f32 * act_f32, axis=-1, keepdims=True) + 1e-06)
    normed = act_f32 * inv_rms
    cols_space = spatial_cols(jax.nn.silu(normed).astype(jnp.bfloat16))
    cols_time = temporal_cols(jax.nn.silu(middle).astype(jnp.bfloat16))
    back_time = lax.dot_general(
        flatten_cells(grad_out),
        w_temporal,
        (((1,), (1,)), ((), ())),
        preferred_element_type=jnp.float32,
    )
    time_back = temporal_fold(back_time.reshape(section_in.shape[:-1] + (3 * channels,)), channels)
    grad_mid = (time_back * silu_slope(middle)).astype(jnp.bfloat16)
    back_space = lax.dot_general(
        flatten_cells(grad_mid),
        w_spatial,
        (((1,), (1,)), ((), ())),
        preferred_element_type=jnp.float32,
    )
    space_back = spatial_fold(back_space.reshape(section_in.shape[:-1] + (9 * channels,)), channels)
    grad_norm = space_back * silu_slope(normed)
    grad_act = inv_rms * grad_norm - act_f32 * (inv_rms * inv_rms * inv_rms) * jnp.mean(
        grad_norm * act_f32, axis=-1, keepdims=True
    )
    grad_in = (grad_out.astype(jnp.float32) + grad_act).astype(jnp.bfloat16)
    return (cols_space, grad_mid, cols_time, grad_in)


def kernel_term(columns, grads):
    return lax.dot_general(
        flatten_cells(columns),
        flatten_cells(grads),
        (((0,), (0,)), ((), ())),
        preferred_element_type=jnp.float32,
    )


def reduce_over_dp(packed):
    cores = lax.axis_size("core")
    core_idx = lax.axis_index("core")
    by_core = packed.reshape(-1, cores, *packed.shape[1:])
    keep = lax.dynamic_index_in_dim(by_core, core_idx, 1, keepdims=False)
    send = lax.dynamic_index_in_dim(by_core, cores - 1 - core_idx, 1, keepdims=False)
    got = lax.ppermute(send.astype(jnp.bfloat16), "core", [(0, 1), (1, 0)])
    pair_sum = (keep + got.astype(jnp.float32)).astype(jnp.bfloat16)
    gathered = lax.all_to_all(pair_sum, "chip", 0, 0, tiled=True)
    return jnp.sum(gathered.astype(jnp.float32), axis=0)


def local(latents, cotangent, spatial_kernels, temporal_kernels):
    w_spatial = spatial_kernels[0]
    w_temporal = temporal_kernels[0]
    micro_count = latents.shape[0]
    section_count = lax.axis_size("section")
    replicas = lax.axis_size("chip") * lax.axis_size("core")
    section_idx = lax.axis_index("section")
    is_first = section_idx == 0
    is_last = section_idx == section_count - 1
    bwd_first = section_count - 1
    tick_count = micro_count + 2 * section_count - 2
    empty_act = jnp.zeros(latents.shape[1:], jnp.bfloat16)
    stash_in = jnp.zeros((tick_count,) + latents.shape[1:], jnp.bfloat16)
    stash_mid = jnp.zeros((tick_count,) + latents.shape[1:], jnp.float32)
    hold_space = jnp.zeros(w_spatial.shape, jnp.float32)
    hold_time = jnp.zeros(w_temporal.shape, jnp.float32)

    def tick_body(tick, carry):
        recv_act, grad_prev, stash_in, stash_mid, hold_space, hold_time = carry
        recv_grad = from_behind(grad_prev, "section", -1)
        fresh_in = lax.dynamic_index_in_dim(
            latents, jnp.minimum(tick, micro_count - 1), 0, keepdims=False
        )
        section_in = jnp.where(is_first, fresh_in, recv_act)
        section_out, middle = section_forward(section_in, w_spatial, w_temporal)
        stash_in = lax.dynamic_update_index_in_dim(stash_in, section_in, tick, 0)
        stash_mid = lax.dynamic_update_index_in_dim(stash_mid, middle, tick, 0)
        recv_next = from_behind(section_out, "section", 1)
        fresh_grad = lax.dynamic_index_in_dim(
            cotangent, jnp.clip(tick - bwd_first, 0, micro_count - 1), 0, keepdims=False
        )
        grad_now = jnp.where(is_last, fresh_grad, recv_grad)
        micro_idx = tick - 2 * (section_count - 1) + section_idx
        active = (micro_idx >= 0) & (micro_idx < micro_count)
        slot_idx = jnp.clip(micro_idx + section_idx, 0, tick_count - 1)
        section_in_b = lax.dynamic_index_in_dim(stash_in, slot_idx, 0, keepdims=False)
        middle_b = lax.dynamic_index_in_dim(stash_mid, slot_idx, 0, keepdims=False)
        cols_space, grad_mid, cols_time, grad_in = section_backward(
            grad_now, section_in_b, middle_b, w_spatial, w_temporal
        )
        active_weight = active.astype(jnp.float32)
        hold_space = hold_space + active_weight * kernel_term(cols_space, grad_mid)
        hold_time = hold_time + active_weight * kernel_term(cols_time, grad_now)
        return (recv_next, grad_in, stash_in, stash_mid, hold_space, hold_time)

    carry = (empty_act, empty_act, stash_in, stash_mid, hold_space, hold_time)
    carry = lax.fori_loop(0, tick_count, tick_body, carry)
    hold_space, hold_time = carry[4], carry[5]
    rows_space = w_spatial.shape[0] // replicas
    rows_time = w_temporal.shape[0] // replicas
    packed = jnp.concatenate(
        [
            hold_space.reshape(replicas, rows_space, -1),
            hold_time.reshape(replicas, rows_time, -1),
        ],
        axis=1,
    )
    share = reduce_over_dp(packed)
    share_space, share_time = (share[:rows_space], share[rows_space:])
    cells = (
        micro_count
        * replicas
        * latents.shape[1]
        * latents.shape[2]
        * latents.shape[3]
        * latents.shape[4]
    )
    grad_scale = 1.0 / math.sqrt(cells)
    return ((grad_scale * share_space)[None], (grad_scale * share_time)[None])


def solution(mesh):
    cores = 2
    chip_mesh = Mesh(
        np.asarray(mesh.devices).reshape(mesh.shape["section"], mesh.shape["dp"] // cores, cores),
        ("section", "chip", "core"),
    )
    dp = ("chip", "core")
    in_specs = (
        P(None, dp, None, None, None, None),
        P(None, dp, None, None, None, None),
        P("section", None, None),
        P("section", None, None),
    )
    out_specs = (P("section", dp, None), P("section", dp, None))
    return jax.shard_map(local, mesh=chip_mesh, in_specs=in_specs, out_specs=out_specs, check_vma=False)
```

```python
import math

import jax
import jax.numpy as jnp
from jax import lax
import numpy as np
from jax.sharding import Mesh, PartitionSpec as P


def from_behind(value, axis, steps):
    count = lax.axis_size(axis)
    first, last = (max(0, -steps), min(count, count - steps))
    return lax.ppermute(value, axis, [(source, source + steps) for source in range(first, last)])


def silu_slope(value):
    sig = jax.nn.sigmoid(value)
    return sig * (1.0 + value * (1.0 - sig))


def flatten_cells(array):
    return array.reshape(-1, array.shape[-1])


def spatial_cols(source):
    height, width = (source.shape[2], source.shape[3])
    padded = jnp.pad(source, ((0, 0), (0, 0), (1, 1), (1, 1), (0, 0)))
    return jnp.concatenate(
        [
            padded[:, :, row_tap : row_tap + height, col_tap : col_tap + width, :]
            for row_tap in range(3)
            for col_tap in range(3)
        ],
        axis=-1,
    )


def temporal_cols(source):
    frames = source.shape[1]
    padded = jnp.pad(source, ((0, 0), (2, 0), (0, 0), (0, 0), (0, 0)))
    return jnp.concatenate([padded[:, tap : tap + frames] for tap in range(3)], axis=-1)


def spatial_fold(columns, channels):
    height, width = (columns.shape[2], columns.shape[3])
    padded = jnp.pad(columns, ((0, 0), (0, 0), (1, 1), (1, 1), (0, 0)))
    total = jnp.zeros(columns.shape[:-1] + (channels,), jnp.float32)
    for row_tap in range(3):
        for col_tap in range(3):
            tap = row_tap * 3 + col_tap
            total = (
                total
                + padded[
                    :,
                    :,
                    2 - row_tap : 2 - row_tap + height,
                    2 - col_tap : 2 - col_tap + width,
                    tap * channels : (tap + 1) * channels,
                ]
            )
    return total


def temporal_fold(columns, channels):
    frames = columns.shape[1]
    padded = jnp.pad(columns, ((0, 0), (0, 2), (0, 0), (0, 0), (0, 0)))
    total = jnp.zeros(columns.shape[:-1] + (channels,), jnp.float32)
    for tap in range(3):
        total = (
            total
            + padded[:, 2 - tap : 2 - tap + frames, :, :, tap * channels : (tap + 1) * channels]
        )
    return total


def section_forward(section_in, w_spatial, w_temporal):
    act_f32 = section_in.astype(jnp.float32)
    inv_rms = lax.rsqrt(jnp.mean(act_f32 * act_f32, axis=-1, keepdims=True) + 1e-06)
    silu_one = jax.nn.silu(act_f32 * inv_rms).astype(jnp.bfloat16)
    cols_space = spatial_cols(silu_one)
    middle = jnp.dot(
        flatten_cells(cols_space), w_spatial, preferred_element_type=jnp.float32
    ).reshape(section_in.shape)
    silu_two = jax.nn.silu(middle).astype(jnp.bfloat16)
    cols_time = temporal_cols(silu_two)
    branch = jnp.dot(
        flatten_cells(cols_time), w_temporal, preferred_element_type=jnp.float32
    ).reshape(section_in.shape)
    return ((act_f32 + branch).astype(jnp.bfloat16), middle)


def section_recompute(section_in, w_spatial):
    act_f32 = section_in.astype(jnp.float32)
    inv_rms = lax.rsqrt(jnp.mean(act_f32 * act_f32, axis=-1, keepdims=True) + 1e-06)
    normed = act_f32 * inv_rms
    cols_space = spatial_cols(jax.nn.silu(normed).astype(jnp.bfloat16))
    middle = jnp.dot(
        flatten_cells(cols_space), w_spatial, preferred_element_type=jnp.float32
    ).reshape(section_in.shape)
    return act_f32, inv_rms, normed, cols_space, middle


def section_backward(grad_out, act_f32, inv_rms, normed, middle, w_spatial, w_temporal):
    channels = act_f32.shape[-1]
    cols_time = temporal_cols(jax.nn.silu(middle).astype(jnp.bfloat16))
    back_time = lax.dot_general(
        flatten_cells(grad_out),
        w_temporal,
        (((1,), (1,)), ((), ())),
        preferred_element_type=jnp.float32,
    )
    time_back = temporal_fold(back_time.reshape(act_f32.shape[:-1] + (3 * channels,)), channels)
    grad_mid = (time_back * silu_slope(middle)).astype(jnp.bfloat16)
    back_space = lax.dot_general(
        flatten_cells(grad_mid),
        w_spatial,
        (((1,), (1,)), ((), ())),
        preferred_element_type=jnp.float32,
    )
    space_back = spatial_fold(back_space.reshape(act_f32.shape[:-1] + (9 * channels,)), channels)
    grad_norm = space_back * silu_slope(normed)
    grad_act = inv_rms * grad_norm - act_f32 * (inv_rms * inv_rms * inv_rms) * jnp.mean(
        grad_norm * act_f32, axis=-1, keepdims=True
    )
    grad_in = (grad_out.astype(jnp.float32) + grad_act).astype(jnp.bfloat16)
    return (grad_mid, cols_time, grad_in)


def kernel_term(columns, grads):
    return lax.dot_general(
        flatten_cells(columns),
        flatten_cells(grads),
        (((0,), (0,)), ((), ())),
        preferred_element_type=jnp.float32,
    )


def reduce_over_dp(packed):
    cores = lax.axis_size("core")
    core_idx = lax.axis_index("core")
    by_core = packed.reshape(-1, cores, *packed.shape[1:])
    keep = lax.dynamic_index_in_dim(by_core, core_idx, 1, keepdims=False)
    send = lax.dynamic_index_in_dim(by_core, cores - 1 - core_idx, 1, keepdims=False)
    got = lax.ppermute(send.astype(jnp.bfloat16), "core", [(0, 1), (1, 0)])
    pair_sum = (keep + got.astype(jnp.float32)).astype(jnp.bfloat16)
    gathered = lax.all_to_all(pair_sum, "chip", 0, 0, tiled=True)
    return jnp.sum(gathered.astype(jnp.float32), axis=0)


def local(latents, cotangent, spatial_kernels, temporal_kernels):
    w_spatial = spatial_kernels[0]
    w_temporal = temporal_kernels[0]
    micro_count = latents.shape[0]
    section_count = lax.axis_size("section")
    replicas = lax.axis_size("chip") * lax.axis_size("core")
    section_idx = lax.axis_index("section")
    is_first = section_idx == 0
    is_last = section_idx == section_count - 1
    fwd_last = micro_count + section_count - 2
    bwd_first = section_count - 1
    tick_count = micro_count + 2 * section_count - 2
    empty_act = jnp.zeros(latents.shape[1:], jnp.bfloat16)
    stash_in = jnp.zeros((fwd_last + 1,) + latents.shape[1:], jnp.bfloat16)
    hold_space = jnp.zeros(w_spatial.shape, jnp.float32)
    hold_time = jnp.zeros(w_temporal.shape, jnp.float32)
    recv_act = empty_act
    grad_in = None
    for tick in range(tick_count):
        if grad_in is not None:
            recv_grad = from_behind(grad_in, "section", -1)
        if tick <= fwd_last:
            fresh_in = latents[tick] if tick < micro_count else empty_act
            section_in = jnp.where(is_first, fresh_in, recv_act)
            section_out, _ = section_forward(section_in, w_spatial, w_temporal)
            stash_in = stash_in.at[tick].set(section_in)
            if tick + 1 <= fwd_last:
                recv_act = from_behind(section_out, "section", 1)
        if tick >= bwd_first:
            fresh_idx = tick - bwd_first
            fresh_grad = cotangent[fresh_idx] if fresh_idx < micro_count else empty_act
            grad_now = jnp.where(is_last, fresh_grad, recv_grad) if tick > bwd_first else fresh_grad
            micro_idx = tick - 2 * (section_count - 1) + section_idx
            active = (micro_idx >= 0) & (micro_idx < micro_count)
            slot_idx = jnp.clip(micro_idx + section_idx, 0, fwd_last)
            section_in_b = lax.dynamic_index_in_dim(stash_in, slot_idx, 0, keepdims=False)
            act_f32, inv_rms, normed, cols_space, middle_b = section_recompute(
                section_in_b, w_spatial
            )
            grad_mid, cols_time, grad_in = section_backward(
                grad_now, act_f32, inv_rms, normed, middle_b, w_spatial, w_temporal
            )
            active_weight = active.astype(jnp.float32)
            hold_space = hold_space + active_weight * kernel_term(cols_space, grad_mid)
            hold_time = hold_time + active_weight * kernel_term(cols_time, grad_now)
            if tick == tick_count - 2:
                hold_space, hold_time = lax.optimization_barrier((hold_space, hold_time))
            if tick + 1 >= tick_count:
                grad_in = None
    rows_space = w_spatial.shape[0] // replicas
    rows_time = w_temporal.shape[0] // replicas
    packed = jnp.concatenate(
        [
            hold_space.reshape(replicas, rows_space, -1),
            hold_time.reshape(replicas, rows_time, -1),
        ],
        axis=1,
    )
    share = reduce_over_dp(packed)
    share_space, share_time = (share[:rows_space], share[rows_space:])
    cells = (
        micro_count
        * replicas
        * latents.shape[1]
        * latents.shape[2]
        * latents.shape[3]
        * latents.shape[4]
    )
    grad_scale = 1.0 / math.sqrt(cells)
    return ((grad_scale * share_space)[None], (grad_scale * share_time)[None])


def solution(mesh):
    cores = 2
    chip_mesh = Mesh(
        np.asarray(mesh.devices).reshape(mesh.shape["section"], mesh.shape["dp"] // cores, cores),
        ("section", "chip", "core"),
    )
    dp = ("chip", "core")
    in_specs = (
        P(None, dp, None, None, None, None),
        P(None, dp, None, None, None, None),
        P("section", None, None),
        P("section", None, None),
    )
    out_specs = (P("section", dp, None), P("section", dp, None))
    return jax.shard_map(local, mesh=chip_mesh, in_specs=in_specs, out_specs=out_specs, check_vma=False)
```

```python
import math

import jax
import jax.numpy as jnp
from jax import lax
import numpy as np
from jax.sharding import Mesh, PartitionSpec as P


def from_behind(value, axis, steps):
    count = lax.axis_size(axis)
    first, last = (max(0, -steps), min(count, count - steps))
    return lax.ppermute(value, axis, [(source, source + steps) for source in range(first, last)])


def silu_slope(value):
    sig = jax.nn.sigmoid(value)
    return sig * (1.0 + value * (1.0 - sig))


def flatten_cells(array):
    return array.reshape(-1, array.shape[-1])


def spatial_cols(source):
    height, width = (source.shape[2], source.shape[3])
    padded = jnp.pad(source, ((0, 0), (0, 0), (1, 1), (1, 1), (0, 0)))
    return jnp.concatenate(
        [
            padded[:, :, row_tap : row_tap + height, col_tap : col_tap + width, :]
            for row_tap in range(3)
            for col_tap in range(3)
        ],
        axis=-1,
    )


def temporal_cols(source):
    frames = source.shape[1]
    padded = jnp.pad(source, ((0, 0), (2, 0), (0, 0), (0, 0), (0, 0)))
    return jnp.concatenate([padded[:, tap : tap + frames] for tap in range(3)], axis=-1)


def spatial_fold(columns, channels):
    height, width = (columns.shape[2], columns.shape[3])
    padded = jnp.pad(columns, ((0, 0), (0, 0), (1, 1), (1, 1), (0, 0)))
    total = jnp.zeros(columns.shape[:-1] + (channels,), jnp.float32)
    for row_tap in range(3):
        for col_tap in range(3):
            tap = row_tap * 3 + col_tap
            total = (
                total
                + padded[
                    :,
                    :,
                    2 - row_tap : 2 - row_tap + height,
                    2 - col_tap : 2 - col_tap + width,
                    tap * channels : (tap + 1) * channels,
                ]
            )
    return total


def temporal_fold(columns, channels):
    frames = columns.shape[1]
    padded = jnp.pad(columns, ((0, 0), (0, 2), (0, 0), (0, 0), (0, 0)))
    total = jnp.zeros(columns.shape[:-1] + (channels,), jnp.float32)
    for tap in range(3):
        total = (
            total
            + padded[:, 2 - tap : 2 - tap + frames, :, :, tap * channels : (tap + 1) * channels]
        )
    return total


def section_forward(section_in, w_spatial, w_temporal):
    act_f32 = section_in.astype(jnp.float32)
    inv_rms = lax.rsqrt(jnp.mean(act_f32 * act_f32, axis=-1, keepdims=True) + 1e-06)
    silu_one = jax.nn.silu(act_f32 * inv_rms).astype(jnp.bfloat16)
    cols_space = spatial_cols(silu_one)
    middle = jnp.dot(
        flatten_cells(cols_space), w_spatial, preferred_element_type=jnp.float32
    ).reshape(section_in.shape)
    silu_two = jax.nn.silu(middle).astype(jnp.bfloat16)
    cols_time = temporal_cols(silu_two)
    branch = jnp.dot(
        flatten_cells(cols_time), w_temporal, preferred_element_type=jnp.float32
    ).reshape(section_in.shape)
    return ((act_f32 + branch).astype(jnp.bfloat16), middle)


def section_backward(grad_out, section_in, middle, w_spatial, w_temporal):
    channels = section_in.shape[-1]
    act_f32 = section_in.astype(jnp.float32)
    inv_rms = lax.rsqrt(jnp.mean(act_f32 * act_f32, axis=-1, keepdims=True) + 1e-06)
    normed = act_f32 * inv_rms
    cols_space = spatial_cols(jax.nn.silu(normed).astype(jnp.bfloat16))
    cols_time = temporal_cols(jax.nn.silu(middle).astype(jnp.bfloat16))
    back_time = lax.dot_general(
        flatten_cells(grad_out),
        w_temporal,
        (((1,), (1,)), ((), ())),
        preferred_element_type=jnp.float32,
    )
    time_back = temporal_fold(back_time.reshape(section_in.shape[:-1] + (3 * channels,)), channels)
    grad_mid = (time_back * silu_slope(middle)).astype(jnp.bfloat16)
    back_space = lax.dot_general(
        flatten_cells(grad_mid),
        w_spatial,
        (((1,), (1,)), ((), ())),
        preferred_element_type=jnp.float32,
    )
    space_back = spatial_fold(back_space.reshape(section_in.shape[:-1] + (9 * channels,)), channels)
    grad_norm = space_back * silu_slope(normed)
    grad_act = inv_rms * grad_norm - act_f32 * (inv_rms * inv_rms * inv_rms) * jnp.mean(
        grad_norm * act_f32, axis=-1, keepdims=True
    )
    grad_in = (grad_out.astype(jnp.float32) + grad_act).astype(jnp.bfloat16)
    return (cols_space, grad_mid, cols_time, grad_in)


def kernel_term(columns, grads):
    return lax.dot_general(
        flatten_cells(columns),
        flatten_cells(grads),
        (((0,), (0,)), ((), ())),
        preferred_element_type=jnp.float32,
    )


def reduce_over_dp(packed):
    cores = lax.axis_size("core")
    core_idx = lax.axis_index("core")
    by_core = packed.reshape(-1, cores, *packed.shape[1:])
    keep = lax.dynamic_index_in_dim(by_core, core_idx, 1, keepdims=False)
    send = lax.dynamic_index_in_dim(by_core, cores - 1 - core_idx, 1, keepdims=False)
    got = lax.ppermute(send.astype(jnp.bfloat16), "core", [(0, 1), (1, 0)])
    pair_sum = (keep + got.astype(jnp.float32)).astype(jnp.bfloat16)
    gathered = lax.all_to_all(pair_sum, "chip", 0, 0, tiled=True)
    return jnp.sum(gathered.astype(jnp.float32), axis=0)


def local(latents, cotangent, spatial_kernels, temporal_kernels):
    w_spatial = spatial_kernels[0]
    w_temporal = temporal_kernels[0]
    micro_count = latents.shape[0]
    section_count = lax.axis_size("section")
    replicas = lax.axis_size("chip") * lax.axis_size("core")
    section_idx = lax.axis_index("section")
    is_first = section_idx == 0
    is_last = section_idx == section_count - 1
    fwd_last = micro_count + section_count - 2
    bwd_first = section_count - 1
    tick_count = micro_count + 2 * section_count - 2
    empty_act = jnp.zeros(latents.shape[1:], jnp.bfloat16)
    stash_in = jnp.zeros((fwd_last + 1,) + latents.shape[1:], jnp.bfloat16)
    stash_mid = jnp.zeros((fwd_last + 1,) + latents.shape[1:], jnp.float32)
    hold_space = jnp.zeros(w_spatial.shape, jnp.float32)
    hold_time = jnp.zeros(w_temporal.shape, jnp.float32)
    recv_act = empty_act
    grad_in = None
    for tick in range(tick_count):
        if grad_in is not None:
            recv_grad = from_behind(grad_in, "section", -1)
        if tick <= fwd_last:
            fresh_in = latents[tick] if tick < micro_count else empty_act
            section_in = jnp.where(is_first, fresh_in, recv_act)
            section_out, middle = section_forward(section_in, w_spatial, w_temporal)
            stash_in = stash_in.at[tick].set(section_in)
            stash_mid = stash_mid.at[tick].set(middle)
            if tick + 1 <= fwd_last:
                recv_act = from_behind(section_out, "section", 1)
        if tick >= bwd_first:
            fresh_idx = tick - bwd_first
            fresh_grad = cotangent[fresh_idx] if fresh_idx < micro_count else empty_act
            grad_now = jnp.where(is_last, fresh_grad, recv_grad) if tick > bwd_first else fresh_grad
            micro_idx = tick - 2 * (section_count - 1) + section_idx
            active = (micro_idx >= 0) & (micro_idx < micro_count)
            slot_idx = jnp.clip(micro_idx + section_idx, 0, fwd_last)
            section_in_b = lax.dynamic_index_in_dim(stash_in, slot_idx, 0, keepdims=False)
            middle_b = lax.dynamic_index_in_dim(stash_mid, slot_idx, 0, keepdims=False)
            cols_space, grad_mid, cols_time, grad_in = section_backward(
                grad_now, section_in_b, middle_b, w_spatial, w_temporal
            )
            active_weight = active.astype(jnp.float32)
            hold_space = hold_space + active_weight * kernel_term(cols_space, grad_mid)
            hold_time = hold_time + active_weight * kernel_term(cols_time, grad_now)
            if tick + 1 >= tick_count:
                grad_in = None
    rows_space = w_spatial.shape[0] // replicas
    rows_time = w_temporal.shape[0] // replicas
    packed = jnp.concatenate(
        [
            hold_space.reshape(replicas, rows_space, -1),
            hold_time.reshape(replicas, rows_time, -1),
        ],
        axis=1,
    )
    share = reduce_over_dp(packed)
    share_space, share_time = (share[:rows_space], share[rows_space:])
    cells = (
        micro_count
        * replicas
        * latents.shape[1]
        * latents.shape[2]
        * latents.shape[3]
        * latents.shape[4]
    )
    grad_scale = 1.0 / math.sqrt(cells)
    return ((grad_scale * share_space)[None], (grad_scale * share_time)[None])


def solution(mesh):
    cores = 2
    chip_mesh = Mesh(
        np.asarray(mesh.devices).reshape(mesh.shape["section"], mesh.shape["dp"] // cores, cores),
        ("section", "chip", "core"),
    )
    dp = ("chip", "core")
    in_specs = (
        P(None, dp, None, None, None, None),
        P(None, dp, None, None, None, None),
        P("section", None, None),
        P("section", None, None),
    )
    out_specs = (P("section", dp, None), P("section", dp, None))
    return jax.shard_map(local, mesh=chip_mesh, in_specs=in_specs, out_specs=out_specs, check_vma=False)
```

```python
import math

import jax
import jax.numpy as jnp
from jax import lax
import numpy as np
from jax.sharding import Mesh, PartitionSpec as P


def from_behind(value, axis, steps):
    count = lax.axis_size(axis)
    first, last = (max(0, -steps), min(count, count - steps))
    return lax.ppermute(value, axis, [(source, source + steps) for source in range(first, last)])


def silu_slope(value):
    sig = jax.nn.sigmoid(value)
    return sig * (1.0 + value * (1.0 - sig))


def flatten_cells(array):
    return array.reshape(-1, array.shape[-1])


def spatial_cols(source):
    height, width = (source.shape[2], source.shape[3])
    padded = jnp.pad(source, ((0, 0), (0, 0), (1, 1), (1, 1), (0, 0)))
    return jnp.concatenate(
        [
            padded[:, :, row_tap : row_tap + height, col_tap : col_tap + width, :]
            for row_tap in range(3)
            for col_tap in range(3)
        ],
        axis=-1,
    )


def temporal_cols(source):
    frames = source.shape[1]
    padded = jnp.pad(source, ((0, 0), (2, 0), (0, 0), (0, 0), (0, 0)))
    return jnp.concatenate([padded[:, tap : tap + frames] for tap in range(3)], axis=-1)


def temporal_fold(columns, channels):
    frames = columns.shape[1]
    padded = jnp.pad(columns, ((0, 0), (0, 2), (0, 0), (0, 0), (0, 0)))
    total = jnp.zeros(columns.shape[:-1] + (channels,), jnp.float32)
    for tap in range(3):
        total = (
            total
            + padded[:, 2 - tap : 2 - tap + frames, :, :, tap * channels : (tap + 1) * channels]
        )
    return total


def section_forward(section_in, w_spatial, w_temporal):
    act_f32 = section_in.astype(jnp.float32)
    inv_rms = lax.rsqrt(jnp.mean(act_f32 * act_f32, axis=-1, keepdims=True) + 1e-06)
    silu_one = jax.nn.silu(act_f32 * inv_rms).astype(jnp.bfloat16)
    cols_space = spatial_cols(silu_one)
    middle = jnp.dot(
        flatten_cells(cols_space), w_spatial, preferred_element_type=jnp.float32
    ).reshape(section_in.shape)
    silu_two = jax.nn.silu(middle).astype(jnp.bfloat16)
    cols_time = temporal_cols(silu_two)
    branch = jnp.dot(
        flatten_cells(cols_time), w_temporal, preferred_element_type=jnp.float32
    ).reshape(section_in.shape)
    return ((act_f32 + branch).astype(jnp.bfloat16), middle)


def section_backward(grad_out, section_in, middle, w_spatial_flip, w_temporal):
    channels = section_in.shape[-1]
    act_f32 = section_in.astype(jnp.float32)
    inv_rms = lax.rsqrt(jnp.mean(act_f32 * act_f32, axis=-1, keepdims=True) + 1e-06)
    normed = act_f32 * inv_rms
    cols_space = spatial_cols(jax.nn.silu(normed).astype(jnp.bfloat16))
    cols_time = temporal_cols(jax.nn.silu(middle).astype(jnp.bfloat16))
    back_time = lax.dot_general(
        flatten_cells(grad_out),
        w_temporal,
        (((1,), (1,)), ((), ())),
        preferred_element_type=jnp.float32,
    )
    time_back = temporal_fold(back_time.reshape(section_in.shape[:-1] + (3 * channels,)), channels)
    grad_mid = (time_back * silu_slope(middle)).astype(jnp.bfloat16)
    height, width = (section_in.shape[2], section_in.shape[3])
    space_back = lax.conv_general_dilated(
        grad_mid.reshape(-1, height, width, channels),
        w_spatial_flip,
        (1, 1),
        ((1, 1), (1, 1)),
        dimension_numbers=("NHWC", "HWIO", "NHWC"),
        preferred_element_type=jnp.float32,
    ).reshape(section_in.shape)
    grad_norm = space_back * silu_slope(normed)
    grad_act = inv_rms * grad_norm - act_f32 * (inv_rms * inv_rms * inv_rms) * jnp.mean(
        grad_norm * act_f32, axis=-1, keepdims=True
    )
    grad_in = (grad_out.astype(jnp.float32) + grad_act).astype(jnp.bfloat16)
    return (cols_space, grad_mid, cols_time, grad_in)


def kernel_term(columns, grads):
    return lax.dot_general(
        flatten_cells(columns),
        flatten_cells(grads),
        (((0,), (0,)), ((), ())),
        preferred_element_type=jnp.float32,
    )


def reduce_over_dp(packed):
    cores = lax.axis_size("core")
    core_idx = lax.axis_index("core")
    by_core = packed.reshape(-1, cores, *packed.shape[1:])
    keep = lax.dynamic_index_in_dim(by_core, core_idx, 1, keepdims=False)
    send = lax.dynamic_index_in_dim(by_core, cores - 1 - core_idx, 1, keepdims=False)
    got = lax.ppermute(send.astype(jnp.bfloat16), "core", [(0, 1), (1, 0)])
    pair_sum = (keep + got.astype(jnp.float32)).astype(jnp.bfloat16)
    gathered = lax.all_to_all(pair_sum, "chip", 0, 0, tiled=True)
    return jnp.sum(gathered.astype(jnp.float32), axis=0)


def local(latents, cotangent, spatial_kernels, temporal_kernels):
    w_spatial = spatial_kernels[0]
    w_temporal = temporal_kernels[0]
    channels = w_spatial.shape[-1]
    w_spatial_flip = w_spatial.reshape(3, 3, -1, channels)[::-1, ::-1].transpose(0, 1, 3, 2)
    micro_count = latents.shape[0]
    section_count = lax.axis_size("section")
    replicas = lax.axis_size("chip") * lax.axis_size("core")
    section_idx = lax.axis_index("section")
    is_first = section_idx == 0
    is_last = section_idx == section_count - 1
    fwd_last = micro_count + section_count - 2
    bwd_first = section_count - 1
    tick_count = micro_count + 2 * section_count - 2
    empty_act = jnp.zeros(latents.shape[1:], jnp.bfloat16)
    stash_in = jnp.zeros((fwd_last + 1,) + latents.shape[1:], jnp.bfloat16)
    stash_mid = jnp.zeros((fwd_last + 1,) + latents.shape[1:], jnp.float32)
    hold_space = jnp.zeros(w_spatial.shape, jnp.float32)
    hold_time = jnp.zeros(w_temporal.shape, jnp.float32)
    recv_act = empty_act
    grad_in = None
    for tick in range(tick_count):
        if grad_in is not None:
            recv_grad = from_behind(grad_in, "section", -1)
        if tick <= fwd_last:
            fresh_in = latents[tick] if tick < micro_count else empty_act
            section_in = jnp.where(is_first, fresh_in, recv_act)
            section_out, middle = section_forward(section_in, w_spatial, w_temporal)
            stash_in = stash_in.at[tick].set(section_in)
            stash_mid = stash_mid.at[tick].set(middle)
            if tick + 1 <= fwd_last:
                recv_act = from_behind(section_out, "section", 1)
        if tick >= bwd_first:
            fresh_idx = tick - bwd_first
            fresh_grad = cotangent[fresh_idx] if fresh_idx < micro_count else empty_act
            grad_now = jnp.where(is_last, fresh_grad, recv_grad) if tick > bwd_first else fresh_grad
            micro_idx = tick - 2 * (section_count - 1) + section_idx
            active = (micro_idx >= 0) & (micro_idx < micro_count)
            slot_idx = jnp.clip(micro_idx + section_idx, 0, fwd_last)
            section_in_b = lax.dynamic_index_in_dim(stash_in, slot_idx, 0, keepdims=False)
            middle_b = lax.dynamic_index_in_dim(stash_mid, slot_idx, 0, keepdims=False)
            cols_space, grad_mid, cols_time, grad_in = section_backward(
                grad_now, section_in_b, middle_b, w_spatial_flip, w_temporal
            )
            active_weight = active.astype(jnp.float32)
            hold_space = hold_space + active_weight * kernel_term(cols_space, grad_mid)
            hold_time = hold_time + active_weight * kernel_term(cols_time, grad_now)
            if tick + 1 >= tick_count:
                grad_in = None
    rows_space = w_spatial.shape[0] // replicas
    rows_time = w_temporal.shape[0] // replicas
    packed = jnp.concatenate(
        [
            hold_space.reshape(replicas, rows_space, -1),
            hold_time.reshape(replicas, rows_time, -1),
        ],
        axis=1,
    )
    share = reduce_over_dp(packed)
    share_space, share_time = (share[:rows_space], share[rows_space:])
    cells = (
        micro_count
        * replicas
        * latents.shape[1]
        * latents.shape[2]
        * latents.shape[3]
        * latents.shape[4]
    )
    grad_scale = 1.0 / math.sqrt(cells)
    return ((grad_scale * share_space)[None], (grad_scale * share_time)[None])


def solution(mesh):
    cores = 2
    chip_mesh = Mesh(
        np.asarray(mesh.devices).reshape(mesh.shape["section"], mesh.shape["dp"] // cores, cores),
        ("section", "chip", "core"),
    )
    dp = ("chip", "core")
    in_specs = (
        P(None, dp, None, None, None, None),
        P(None, dp, None, None, None, None),
        P("section", None, None),
        P("section", None, None),
    )
    out_specs = (P("section", dp, None), P("section", dp, None))
    return jax.shard_map(local, mesh=chip_mesh, in_specs=in_specs, out_specs=out_specs, check_vma=False)
```

```python
import math

import jax
import jax.numpy as jnp
from jax import lax
import numpy as np
from jax.sharding import Mesh, PartitionSpec as P


def from_behind(value, axis, steps):
    count = lax.axis_size(axis)
    return lax.ppermute(value, axis, [(source, (source + steps) % count) for source in range(count)])


def silu_slope(value):
    sig = jax.nn.sigmoid(value)
    return sig * (1.0 + value * (1.0 - sig))


def flatten_cells(array):
    return array.reshape(-1, array.shape[-1])


def spatial_cols(source):
    height, width = (source.shape[2], source.shape[3])
    padded = jnp.pad(source, ((0, 0), (0, 0), (1, 1), (1, 1), (0, 0)))
    return jnp.concatenate(
        [
            padded[:, :, row_tap : row_tap + height, col_tap : col_tap + width, :]
            for row_tap in range(3)
            for col_tap in range(3)
        ],
        axis=-1,
    )


def temporal_cols(source):
    frames = source.shape[1]
    padded = jnp.pad(source, ((0, 0), (2, 0), (0, 0), (0, 0), (0, 0)))
    return jnp.concatenate([padded[:, tap : tap + frames] for tap in range(3)], axis=-1)


def spatial_fold(columns, channels):
    height, width = (columns.shape[2], columns.shape[3])
    padded = jnp.pad(columns, ((0, 0), (0, 0), (1, 1), (1, 1), (0, 0)))
    total = jnp.zeros(columns.shape[:-1] + (channels,), jnp.float32)
    for row_tap in range(3):
        for col_tap in range(3):
            tap = row_tap * 3 + col_tap
            total = (
                total
                + padded[
                    :,
                    :,
                    2 - row_tap : 2 - row_tap + height,
                    2 - col_tap : 2 - col_tap + width,
                    tap * channels : (tap + 1) * channels,
                ]
            )
    return total


def temporal_fold(columns, channels):
    frames = columns.shape[1]
    padded = jnp.pad(columns, ((0, 0), (0, 2), (0, 0), (0, 0), (0, 0)))
    total = jnp.zeros(columns.shape[:-1] + (channels,), jnp.float32)
    for tap in range(3):
        total = (
            total
            + padded[:, 2 - tap : 2 - tap + frames, :, :, tap * channels : (tap + 1) * channels]
        )
    return total


def section_forward(section_in, w_spatial, w_temporal):
    act_f32 = section_in.astype(jnp.float32)
    inv_rms = lax.rsqrt(jnp.mean(act_f32 * act_f32, axis=-1, keepdims=True) + 1e-06)
    silu_one = jax.nn.silu(act_f32 * inv_rms).astype(jnp.bfloat16)
    cols_space = spatial_cols(silu_one)
    middle = jnp.dot(
        flatten_cells(cols_space), w_spatial, preferred_element_type=jnp.float32
    ).reshape(section_in.shape)
    silu_two = jax.nn.silu(middle).astype(jnp.bfloat16)
    cols_time = temporal_cols(silu_two)
    branch = jnp.dot(
        flatten_cells(cols_time), w_temporal, preferred_element_type=jnp.float32
    ).reshape(section_in.shape)
    return ((act_f32 + branch).astype(jnp.bfloat16), middle)


def section_backward(grad_out, section_in, middle, w_spatial, w_temporal):
    channels = section_in.shape[-1]
    act_f32 = section_in.astype(jnp.float32)
    inv_rms = lax.rsqrt(jnp.mean(act_f32 * act_f32, axis=-1, keepdims=True) + 1e-06)
    normed = act_f32 * inv_rms
    cols_space = spatial_cols(jax.nn.silu(normed).astype(jnp.bfloat16))
    cols_time = temporal_cols(jax.nn.silu(middle).astype(jnp.bfloat16))
    back_time = lax.dot_general(
        flatten_cells(grad_out),
        w_temporal,
        (((1,), (1,)), ((), ())),
        preferred_element_type=jnp.float32,
    )
    time_back = temporal_fold(back_time.reshape(section_in.shape[:-1] + (3 * channels,)), channels)
    grad_mid = (time_back * silu_slope(middle)).astype(jnp.bfloat16)
    back_space = lax.dot_general(
        flatten_cells(grad_mid),
        w_spatial,
        (((1,), (1,)), ((), ())),
        preferred_element_type=jnp.float32,
    )
    space_back = spatial_fold(back_space.reshape(section_in.shape[:-1] + (9 * channels,)), channels)
    grad_norm = space_back * silu_slope(normed)
    grad_act = inv_rms * grad_norm - act_f32 * (inv_rms * inv_rms * inv_rms) * jnp.mean(
        grad_norm * act_f32, axis=-1, keepdims=True
    )
    grad_in = (grad_out.astype(jnp.float32) + grad_act).astype(jnp.bfloat16)
    return (cols_space, grad_mid, cols_time, grad_in)


def kernel_term(columns, grads):
    return lax.dot_general(
        flatten_cells(columns),
        flatten_cells(grads),
        (((0,), (0,)), ((), ())),
        preferred_element_type=jnp.float32,
    )


def reduce_over_dp(packed):
    cores = lax.axis_size("core")
    core_idx = lax.axis_index("core")
    by_core = packed.reshape(-1, cores, *packed.shape[1:])
    keep = lax.dynamic_index_in_dim(by_core, core_idx, 1, keepdims=False)
    send = lax.dynamic_index_in_dim(by_core, cores - 1 - core_idx, 1, keepdims=False)
    got = lax.ppermute(send.astype(jnp.bfloat16), "core", [(0, 1), (1, 0)])
    pair_sum = (keep + got.astype(jnp.float32)).astype(jnp.bfloat16)
    gathered = lax.all_to_all(pair_sum, "chip", 0, 0, tiled=True)
    return jnp.sum(gathered.astype(jnp.float32), axis=0)


def local(latents, cotangent, spatial_kernels, temporal_kernels):
    w_spatial = spatial_kernels[0]
    w_temporal = temporal_kernels[0]
    micro_count = latents.shape[0]
    section_count = lax.axis_size("section")
    replicas = lax.axis_size("chip") * lax.axis_size("core")
    section_idx = lax.axis_index("section")
    is_first = section_idx == 0
    is_last = section_idx == section_count - 1
    fwd_last = micro_count + section_count - 2
    bwd_first = section_count - 1
    tick_count = micro_count + 2 * section_count - 2
    empty_act = jnp.zeros(latents.shape[1:], jnp.bfloat16)
    stash_in = jnp.zeros((fwd_last + 1,) + latents.shape[1:], jnp.bfloat16)
    stash_mid = jnp.zeros((fwd_last + 1,) + latents.shape[1:], jnp.float32)
    hold_space = jnp.zeros(w_spatial.shape, jnp.float32)
    hold_time = jnp.zeros(w_temporal.shape, jnp.float32)
    recv_act = empty_act
    grad_in = None
    for tick in range(tick_count):
        if grad_in is not None:
            recv_grad = from_behind(grad_in, "section", -1)
        if tick <= fwd_last:
            fresh_in = latents[tick] if tick < micro_count else empty_act
            section_in = jnp.where(is_first, fresh_in, recv_act)
            section_out, middle = section_forward(section_in, w_spatial, w_temporal)
            stash_in = stash_in.at[tick].set(section_in)
            stash_mid = stash_mid.at[tick].set(middle)
            if tick + 1 <= fwd_last:
                recv_act = from_behind(section_out, "section", 1)
        if tick == tick_count - 1:
            hold_space, hold_time = lax.optimization_barrier((hold_space, hold_time))
        if tick >= bwd_first:
            fresh_idx = tick - bwd_first
            fresh_grad = cotangent[fresh_idx] if fresh_idx < micro_count else empty_act
            grad_now = jnp.where(is_last, fresh_grad, recv_grad) if tick > bwd_first else fresh_grad
            micro_idx = tick - 2 * (section_count - 1) + section_idx
            active = (micro_idx >= 0) & (micro_idx < micro_count)
            slot_idx = jnp.clip(micro_idx + section_idx, 0, fwd_last)
            section_in_b = lax.dynamic_index_in_dim(stash_in, slot_idx, 0, keepdims=False)
            middle_b = lax.dynamic_index_in_dim(stash_mid, slot_idx, 0, keepdims=False)
            cols_space, grad_mid, cols_time, grad_in = section_backward(
                grad_now, section_in_b, middle_b, w_spatial, w_temporal
            )
            active_weight = active.astype(jnp.float32)
            hold_space = hold_space + active_weight * kernel_term(cols_space, grad_mid)
            hold_time = hold_time + active_weight * kernel_term(cols_time, grad_now)
            if tick + 1 >= tick_count:
                grad_in = None
    rows_space = w_spatial.shape[0] // replicas
    rows_time = w_temporal.shape[0] // replicas
    packed = jnp.concatenate(
        [
            hold_space.reshape(replicas, rows_space, -1),
            hold_time.reshape(replicas, rows_time, -1),
        ],
        axis=1,
    )
    share = reduce_over_dp(packed)
    share_space, share_time = (share[:rows_space], share[rows_space:])
    cells = (
        micro_count
        * replicas
        * latents.shape[1]
        * latents.shape[2]
        * latents.shape[3]
        * latents.shape[4]
    )
    grad_scale = 1.0 / math.sqrt(cells)
    return ((grad_scale * share_space)[None], (grad_scale * share_time)[None])


def solution(mesh):
    cores = 2
    chip_mesh = Mesh(
        np.asarray(mesh.devices).reshape(mesh.shape["section"], mesh.shape["dp"] // cores, cores),
        ("section", "chip", "core"),
    )
    dp = ("chip", "core")
    in_specs = (
        P(None, dp, None, None, None, None),
        P(None, dp, None, None, None, None),
        P("section", None, None),
        P("section", None, None),
    )
    out_specs = (P("section", dp, None), P("section", dp, None))
    return jax.shard_map(local, mesh=chip_mesh, in_specs=in_specs, out_specs=out_specs, check_vma=False)
```

```python
import math

import jax
import jax.numpy as jnp
from jax import lax
import numpy as np
from jax.sharding import Mesh, PartitionSpec as P


def from_behind(value, axis, steps):
    count = lax.axis_size(axis)
    return lax.ppermute(value, axis, [(source, (source + steps) % count) for source in range(count)])


def silu_slope(value):
    sig = jax.nn.sigmoid(value)
    return sig * (1.0 + value * (1.0 - sig))


def flatten_cells(array):
    return array.reshape(-1, array.shape[-1])


def spatial_cols(source):
    height, width = (source.shape[2], source.shape[3])
    padded = jnp.pad(source, ((0, 0), (0, 0), (1, 1), (1, 1), (0, 0)))
    return jnp.concatenate(
        [
            padded[:, :, row_tap : row_tap + height, col_tap : col_tap + width, :]
            for row_tap in range(3)
            for col_tap in range(3)
        ],
        axis=-1,
    )


def temporal_cols(source):
    frames = source.shape[1]
    padded = jnp.pad(source, ((0, 0), (2, 0), (0, 0), (0, 0), (0, 0)))
    return jnp.concatenate([padded[:, tap : tap + frames] for tap in range(3)], axis=-1)


def spatial_fold(columns, channels):
    height, width = (columns.shape[2], columns.shape[3])
    padded = jnp.pad(columns, ((0, 0), (0, 0), (1, 1), (1, 1), (0, 0)))
    total = jnp.zeros(columns.shape[:-1] + (channels,), jnp.float32)
    for row_tap in range(3):
        for col_tap in range(3):
            tap = row_tap * 3 + col_tap
            total = (
                total
                + padded[
                    :,
                    :,
                    2 - row_tap : 2 - row_tap + height,
                    2 - col_tap : 2 - col_tap + width,
                    tap * channels : (tap + 1) * channels,
                ]
            )
    return total


def temporal_fold(columns, channels):
    frames = columns.shape[1]
    padded = jnp.pad(columns, ((0, 0), (0, 2), (0, 0), (0, 0), (0, 0)))
    total = jnp.zeros(columns.shape[:-1] + (channels,), jnp.float32)
    for tap in range(3):
        total = (
            total
            + padded[:, 2 - tap : 2 - tap + frames, :, :, tap * channels : (tap + 1) * channels]
        )
    return total


def section_forward(section_in, w_spatial, w_temporal):
    act_f32 = section_in.astype(jnp.float32)
    inv_rms = lax.rsqrt(jnp.mean(act_f32 * act_f32, axis=-1, keepdims=True) + 1e-06)
    silu_one = jax.nn.silu(act_f32 * inv_rms).astype(jnp.bfloat16)
    cols_space = spatial_cols(silu_one)
    middle = jnp.dot(
        flatten_cells(cols_space), w_spatial, preferred_element_type=jnp.float32
    ).reshape(section_in.shape)
    silu_two = jax.nn.silu(middle).astype(jnp.bfloat16)
    cols_time = temporal_cols(silu_two)
    branch = jnp.dot(
        flatten_cells(cols_time), w_temporal, preferred_element_type=jnp.float32
    ).reshape(section_in.shape)
    return ((act_f32 + branch).astype(jnp.bfloat16), middle)


def section_backward(grad_out, section_in, middle, w_spatial, w_temporal):
    channels = section_in.shape[-1]
    act_f32 = section_in.astype(jnp.float32)
    inv_rms = lax.rsqrt(jnp.mean(act_f32 * act_f32, axis=-1, keepdims=True) + 1e-06)
    normed = act_f32 * inv_rms
    cols_space = spatial_cols(jax.nn.silu(normed).astype(jnp.bfloat16))
    cols_time = temporal_cols(jax.nn.silu(middle).astype(jnp.bfloat16))
    back_time = lax.dot_general(
        flatten_cells(grad_out),
        w_temporal,
        (((1,), (1,)), ((), ())),
        preferred_element_type=jnp.float32,
    )
    time_back = temporal_fold(back_time.reshape(section_in.shape[:-1] + (3 * channels,)), channels)
    grad_mid = (time_back * silu_slope(middle)).astype(jnp.bfloat16)
    back_space = lax.dot_general(
        flatten_cells(grad_mid),
        w_spatial,
        (((1,), (1,)), ((), ())),
        preferred_element_type=jnp.float32,
    )
    space_back = spatial_fold(back_space.reshape(section_in.shape[:-1] + (9 * channels,)), channels)
    grad_norm = space_back * silu_slope(normed)
    grad_act = inv_rms * grad_norm - act_f32 * (inv_rms * inv_rms * inv_rms) * jnp.mean(
        grad_norm * act_f32, axis=-1, keepdims=True
    )
    grad_in = (grad_out.astype(jnp.float32) + grad_act).astype(jnp.bfloat16)
    return (cols_space, grad_mid, cols_time, grad_in)


def kernel_term(columns, grads):
    return lax.dot_general(
        flatten_cells(columns),
        flatten_cells(grads),
        (((0,), (0,)), ((), ())),
        preferred_element_type=jnp.float32,
    )


def reduce_over_dp(packed):
    cores = lax.axis_size("core")
    core_idx = lax.axis_index("core")
    by_core = packed.reshape(-1, cores, *packed.shape[1:])
    keep = lax.dynamic_index_in_dim(by_core, core_idx, 1, keepdims=False)
    send = lax.dynamic_index_in_dim(by_core, cores - 1 - core_idx, 1, keepdims=False)
    got = lax.ppermute(send.astype(jnp.bfloat16), "core", [(0, 1), (1, 0)])
    pair_sum = (keep + got.astype(jnp.float32)).astype(jnp.bfloat16)
    gathered = lax.all_to_all(pair_sum, "chip", 0, 0, tiled=True)
    return jnp.sum(gathered.astype(jnp.float32), axis=0)


def local(latents, cotangent, spatial_kernels, temporal_kernels):
    w_spatial = spatial_kernels[0]
    w_temporal = temporal_kernels[0]
    micro_count = latents.shape[0]
    section_count = lax.axis_size("section")
    replicas = lax.axis_size("chip") * lax.axis_size("core")
    section_idx = lax.axis_index("section")
    is_first = section_idx == 0
    is_last = section_idx == section_count - 1
    fwd_last = micro_count + section_count - 2
    bwd_first = section_count - 1
    tick_count = micro_count + 2 * section_count - 2
    empty_act = jnp.zeros(latents.shape[1:], jnp.bfloat16)
    stash_in = jnp.zeros((fwd_last + 1,) + latents.shape[1:], jnp.bfloat16)
    stash_mid = jnp.zeros((fwd_last + 1,) + latents.shape[1:], jnp.float32)
    hold_space = jnp.zeros(w_spatial.shape, jnp.float32)
    hold_time = jnp.zeros(w_temporal.shape, jnp.float32)
    recv_act = empty_act
    grad_in = None
    for tick in range(tick_count):
        if grad_in is not None:
            recv_grad = from_behind(grad_in, "section", -1)
        if tick <= fwd_last:
            fresh_in = latents[tick] if tick < micro_count else empty_act
            section_in = jnp.where(is_first, fresh_in, recv_act)
            section_out, middle = section_forward(section_in, w_spatial, w_temporal)
            stash_in = stash_in.at[tick].set(section_in)
            stash_mid = stash_mid.at[tick].set(middle)
            if 1 <= tick < bwd_first + 1:
                spare = from_behind(section_in, "section", -1)
                section_out = jnp.where(section_idx >= section_count, spare, section_out)
            if tick + 1 <= fwd_last:
                recv_act = from_behind(section_out, "section", 1)
        if tick == tick_count - 1:
            hold_space, hold_time = lax.optimization_barrier((hold_space, hold_time))
        if tick >= bwd_first:
            fresh_idx = tick - bwd_first
            fresh_grad = cotangent[fresh_idx] if fresh_idx < micro_count else empty_act
            grad_now = jnp.where(is_last, fresh_grad, recv_grad) if tick > bwd_first else fresh_grad
            micro_idx = tick - 2 * (section_count - 1) + section_idx
            active = (micro_idx >= 0) & (micro_idx < micro_count)
            slot_idx = jnp.clip(micro_idx + section_idx, 0, fwd_last)
            section_in_b = lax.dynamic_index_in_dim(stash_in, slot_idx, 0, keepdims=False)
            middle_b = lax.dynamic_index_in_dim(stash_mid, slot_idx, 0, keepdims=False)
            cols_space, grad_mid, cols_time, grad_in = section_backward(
                grad_now, section_in_b, middle_b, w_spatial, w_temporal
            )
            active_weight = active.astype(jnp.float32)
            hold_space = hold_space + active_weight * kernel_term(cols_space, grad_mid)
            hold_time = hold_time + active_weight * kernel_term(cols_time, grad_now)
            if tick > fwd_last and tick + 1 < tick_count:
                spare = from_behind(grad_now, "section", 1)
                grad_in = jnp.where(section_idx >= section_count, spare, grad_in)
            if tick + 1 >= tick_count:
                grad_in = None
    rows_space = w_spatial.shape[0] // replicas
    rows_time = w_temporal.shape[0] // replicas
    packed = jnp.concatenate(
        [
            hold_space.reshape(replicas, rows_space, -1),
            hold_time.reshape(replicas, rows_time, -1),
        ],
        axis=1,
    )
    share = reduce_over_dp(packed)
    share_space, share_time = (share[:rows_space], share[rows_space:])
    cells = (
        micro_count
        * replicas
        * latents.shape[1]
        * latents.shape[2]
        * latents.shape[3]
        * latents.shape[4]
    )
    grad_scale = 1.0 / math.sqrt(cells)
    return ((grad_scale * share_space)[None], (grad_scale * share_time)[None])


def solution(mesh):
    cores = 2
    chip_mesh = Mesh(
        np.asarray(mesh.devices).reshape(mesh.shape["section"], mesh.shape["dp"] // cores, cores),
        ("section", "chip", "core"),
    )
    dp = ("chip", "core")
    in_specs = (
        P(None, dp, None, None, None, None),
        P(None, dp, None, None, None, None),
        P("section", None, None),
        P("section", None, None),
    )
    out_specs = (P("section", dp, None), P("section", dp, None))
    return jax.shard_map(local, mesh=chip_mesh, in_specs=in_specs, out_specs=out_specs, check_vma=False)
```

```python
import math

import jax
import jax.numpy as jnp
from jax import lax
import numpy as np
from jax.sharding import Mesh, PartitionSpec as P


def from_behind(value, axis, steps):
    count = lax.axis_size(axis)
    return lax.ppermute(value, axis, [(source, (source + steps) % count) for source in range(count)])


def silu_slope(value):
    sig = jax.nn.sigmoid(value)
    return sig * (1.0 + value * (1.0 - sig))


def flatten_cells(array):
    return array.reshape(-1, array.shape[-1])


def spatial_cols(source):
    height, width = (source.shape[2], source.shape[3])
    padded = jnp.pad(source, ((0, 0), (0, 0), (1, 1), (1, 1), (0, 0)))
    return jnp.concatenate(
        [
            padded[:, :, row_tap : row_tap + height, col_tap : col_tap + width, :]
            for row_tap in range(3)
            for col_tap in range(3)
        ],
        axis=-1,
    )


def temporal_cols(source):
    frames = source.shape[1]
    padded = jnp.pad(source, ((0, 0), (2, 0), (0, 0), (0, 0), (0, 0)))
    return jnp.concatenate([padded[:, tap : tap + frames] for tap in range(3)], axis=-1)


def spatial_fold(columns, channels):
    height, width = (columns.shape[2], columns.shape[3])
    padded = jnp.pad(columns, ((0, 0), (0, 0), (1, 1), (1, 1), (0, 0)))
    total = jnp.zeros(columns.shape[:-1] + (channels,), jnp.float32)
    for row_tap in range(3):
        for col_tap in range(3):
            tap = row_tap * 3 + col_tap
            total = (
                total
                + padded[
                    :,
                    :,
                    2 - row_tap : 2 - row_tap + height,
                    2 - col_tap : 2 - col_tap + width,
                    tap * channels : (tap + 1) * channels,
                ]
            )
    return total


def temporal_fold(columns, channels):
    frames = columns.shape[1]
    padded = jnp.pad(columns, ((0, 0), (0, 2), (0, 0), (0, 0), (0, 0)))
    total = jnp.zeros(columns.shape[:-1] + (channels,), jnp.float32)
    for tap in range(3):
        total = (
            total
            + padded[:, 2 - tap : 2 - tap + frames, :, :, tap * channels : (tap + 1) * channels]
        )
    return total


def section_forward(section_in, w_spatial, w_temporal):
    act_f32 = section_in.astype(jnp.float32)
    inv_rms = lax.rsqrt(jnp.mean(act_f32 * act_f32, axis=-1, keepdims=True) + 1e-06)
    silu_one = jax.nn.silu(act_f32 * inv_rms).astype(jnp.bfloat16)
    cols_space = spatial_cols(silu_one)
    middle = jnp.dot(
        flatten_cells(cols_space), w_spatial, preferred_element_type=jnp.float32
    ).reshape(section_in.shape)
    silu_two = jax.nn.silu(middle).astype(jnp.bfloat16)
    cols_time = temporal_cols(silu_two)
    branch = jnp.dot(
        flatten_cells(cols_time), w_temporal, preferred_element_type=jnp.float32
    ).reshape(section_in.shape)
    return ((act_f32 + branch).astype(jnp.bfloat16), middle)


def section_backward(grad_out, section_in, middle, w_spatial, w_temporal):
    channels = section_in.shape[-1]
    act_f32 = section_in.astype(jnp.float32)
    inv_rms = lax.rsqrt(jnp.mean(act_f32 * act_f32, axis=-1, keepdims=True) + 1e-06)
    normed = act_f32 * inv_rms
    cols_space = spatial_cols(jax.nn.silu(normed).astype(jnp.bfloat16))
    cols_time = temporal_cols(jax.nn.silu(middle).astype(jnp.bfloat16))
    back_time = lax.dot_general(
        flatten_cells(grad_out),
        w_temporal,
        (((1,), (1,)), ((), ())),
        preferred_element_type=jnp.float32,
    )
    time_back = temporal_fold(back_time.reshape(section_in.shape[:-1] + (3 * channels,)), channels)
    grad_mid = (time_back * silu_slope(middle)).astype(jnp.bfloat16)
    back_space = lax.dot_general(
        flatten_cells(grad_mid),
        w_spatial,
        (((1,), (1,)), ((), ())),
        preferred_element_type=jnp.float32,
    )
    space_back = spatial_fold(back_space.reshape(section_in.shape[:-1] + (9 * channels,)), channels)
    grad_norm = space_back * silu_slope(normed)
    grad_act = inv_rms * grad_norm - act_f32 * (inv_rms * inv_rms * inv_rms) * jnp.mean(
        grad_norm * act_f32, axis=-1, keepdims=True
    )
    grad_in = (grad_out.astype(jnp.float32) + grad_act).astype(jnp.bfloat16)
    return (cols_space, grad_mid, cols_time, grad_in)


def kernel_term(columns, grads):
    return lax.dot_general(
        flatten_cells(columns),
        flatten_cells(grads),
        (((0,), (0,)), ((), ())),
        preferred_element_type=jnp.float32,
    )


def reduce_over_dp(packed):
    cores = lax.axis_size("core")
    core_idx = lax.axis_index("core")
    by_core = packed.reshape(-1, cores, *packed.shape[1:])
    keep = lax.dynamic_index_in_dim(by_core, core_idx, 1, keepdims=False)
    send = lax.dynamic_index_in_dim(by_core, cores - 1 - core_idx, 1, keepdims=False)
    got = lax.ppermute(send.astype(jnp.bfloat16), "core", [(0, 1), (1, 0)])
    pair_sum = (keep + got.astype(jnp.float32)).astype(jnp.bfloat16)
    gathered = lax.all_to_all(pair_sum, "chip", 0, 0, tiled=True)
    return gathered


def local(latents, cotangent, spatial_kernels, temporal_kernels):
    w_spatial = spatial_kernels[0]
    w_temporal = temporal_kernels[0]
    micro_count = latents.shape[0]
    section_count = lax.axis_size("section")
    replicas = lax.axis_size("chip") * lax.axis_size("core")
    section_idx = lax.axis_index("section")
    is_first = section_idx == 0
    is_last = section_idx == section_count - 1
    fwd_last = micro_count + section_count - 2
    bwd_first = section_count - 1
    tick_count = micro_count + 2 * section_count - 2
    empty_act = jnp.zeros(latents.shape[1:], jnp.bfloat16)
    stash_in = jnp.zeros((fwd_last + 1,) + latents.shape[1:], jnp.bfloat16)
    stash_mid = jnp.zeros((fwd_last + 1,) + latents.shape[1:], jnp.float32)
    hold_space = jnp.zeros(w_spatial.shape, jnp.float32)
    hold_time = jnp.zeros(w_temporal.shape, jnp.float32)
    recv_act = empty_act
    grad_in = None
    for tick in range(tick_count):
        if grad_in is not None:
            recv_grad = from_behind(grad_in, "section", -1)
        if tick <= fwd_last:
            fresh_in = latents[tick] if tick < micro_count else empty_act
            section_in = jnp.where(is_first, fresh_in, recv_act)
            section_out, middle = section_forward(section_in, w_spatial, w_temporal)
            stash_in = stash_in.at[tick].set(section_in)
            stash_mid = stash_mid.at[tick].set(middle)
            if tick + 1 <= fwd_last:
                recv_act = from_behind(section_out, "section", 1)
        if tick == tick_count - 1:
            hold_space, hold_time = lax.optimization_barrier((hold_space, hold_time))
        if tick >= bwd_first:
            fresh_idx = tick - bwd_first
            fresh_grad = cotangent[fresh_idx] if fresh_idx < micro_count else empty_act
            grad_now = jnp.where(is_last, fresh_grad, recv_grad) if tick > bwd_first else fresh_grad
            micro_idx = tick - 2 * (section_count - 1) + section_idx
            active = (micro_idx >= 0) & (micro_idx < micro_count)
            slot_idx = jnp.clip(micro_idx + section_idx, 0, fwd_last)
            section_in_b = lax.dynamic_index_in_dim(stash_in, slot_idx, 0, keepdims=False)
            middle_b = lax.dynamic_index_in_dim(stash_mid, slot_idx, 0, keepdims=False)
            cols_space, grad_mid, cols_time, grad_in = section_backward(
                grad_now, section_in_b, middle_b, w_spatial, w_temporal
            )
            active_weight = active.astype(jnp.float32)
            hold_space = hold_space + active_weight * kernel_term(cols_space, grad_mid)
            hold_time = hold_time + active_weight * kernel_term(cols_time, grad_now)
            if tick + 1 >= tick_count:
                grad_in = None
    rows_space = w_spatial.shape[0] // replicas
    rows_time = w_temporal.shape[0] // replicas
    packed = jnp.concatenate(
        [
            hold_space.reshape(replicas, rows_space, -1),
            hold_time.reshape(replicas, rows_time, -1),
        ],
        axis=1,
    )
    gathered = reduce_over_dp(packed)
    cells = (
        micro_count
        * replicas
        * latents.shape[1]
        * latents.shape[2]
        * latents.shape[3]
        * latents.shape[4]
    )
    grad_scale = 1.0 / math.sqrt(cells)
    share_space = jnp.sum(gathered[:, :rows_space].astype(jnp.float32), axis=0, keepdims=True)
    share_time = jnp.sum(gathered[:, rows_space:].astype(jnp.float32), axis=0, keepdims=True)
    return (grad_scale * share_space, grad_scale * share_time)


def solution(mesh):
    cores = 2
    chip_mesh = Mesh(
        np.asarray(mesh.devices).reshape(mesh.shape["section"], mesh.shape["dp"] // cores, cores),
        ("section", "chip", "core"),
    )
    dp = ("chip", "core")
    in_specs = (
        P(None, dp, None, None, None, None),
        P(None, dp, None, None, None, None),
        P("section", None, None),
        P("section", None, None),
    )
    out_specs = (P("section", dp, None), P("section", dp, None))
    return jax.shard_map(local, mesh=chip_mesh, in_specs=in_specs, out_specs=out_specs, check_vma=False)
```

```python
import math

import jax
import jax.numpy as jnp
from jax import lax
import numpy as np
from jax.sharding import Mesh, PartitionSpec as P


def from_behind(value, axis, steps):
    count = lax.axis_size(axis)
    return lax.ppermute(value, axis, [(source, (source + steps) % count) for source in range(count)])


def silu_slope(value):
    sig = jax.nn.sigmoid(value)
    return sig * (1.0 + value * (1.0 - sig))


def flatten_cells(array):
    return array.reshape(-1, array.shape[-1])


def spatial_cols(source):
    height, width = (source.shape[2], source.shape[3])
    padded = jnp.pad(source, ((0, 0), (0, 0), (1, 1), (1, 1), (0, 0)))
    return jnp.concatenate(
        [
            padded[:, :, row_tap : row_tap + height, col_tap : col_tap + width, :]
            for row_tap in range(3)
            for col_tap in range(3)
        ],
        axis=-1,
    )


def temporal_cols(source):
    frames = source.shape[1]
    padded = jnp.pad(source, ((0, 0), (2, 0), (0, 0), (0, 0), (0, 0)))
    return jnp.concatenate([padded[:, tap : tap + frames] for tap in range(3)], axis=-1)


def temporal_fold(columns, channels):
    frames = columns.shape[1]
    padded = jnp.pad(columns, ((0, 0), (0, 2), (0, 0), (0, 0), (0, 0)))
    total = jnp.zeros(columns.shape[:-1] + (channels,), jnp.float32)
    for tap in range(3):
        total = (
            total
            + padded[:, 2 - tap : 2 - tap + frames, :, :, tap * channels : (tap + 1) * channels]
        )
    return total


def section_forward(section_in, w_spatial, w_temporal):
    act_f32 = section_in.astype(jnp.float32)
    inv_rms = lax.rsqrt(jnp.mean(act_f32 * act_f32, axis=-1, keepdims=True) + 1e-06)
    silu_one = jax.nn.silu(act_f32 * inv_rms).astype(jnp.bfloat16)
    cols_space = spatial_cols(silu_one)
    middle = jnp.dot(
        flatten_cells(cols_space), w_spatial, preferred_element_type=jnp.float32
    ).reshape(section_in.shape)
    silu_two = jax.nn.silu(middle).astype(jnp.bfloat16)
    cols_time = temporal_cols(silu_two)
    branch = jnp.dot(
        flatten_cells(cols_time), w_temporal, preferred_element_type=jnp.float32
    ).reshape(section_in.shape)
    return ((act_f32 + branch).astype(jnp.bfloat16), middle)


def section_backward(grad_out, section_in, middle, w_spatial_flip, w_temporal):
    channels = section_in.shape[-1]
    act_f32 = section_in.astype(jnp.float32)
    inv_rms = lax.rsqrt(jnp.mean(act_f32 * act_f32, axis=-1, keepdims=True) + 1e-06)
    normed = act_f32 * inv_rms
    cols_space = spatial_cols(jax.nn.silu(normed).astype(jnp.bfloat16))
    cols_time = temporal_cols(jax.nn.silu(middle).astype(jnp.bfloat16))
    back_time = lax.dot_general(
        flatten_cells(grad_out),
        w_temporal,
        (((1,), (1,)), ((), ())),
        preferred_element_type=jnp.float32,
    )
    time_back = temporal_fold(back_time.reshape(section_in.shape[:-1] + (3 * channels,)), channels)
    grad_mid = (time_back * silu_slope(middle)).astype(jnp.bfloat16)
    height, width = (section_in.shape[2], section_in.shape[3])
    space_back = lax.conv_general_dilated(
        grad_mid.reshape(-1, height, width, channels),
        w_spatial_flip,
        (1, 1),
        ((1, 1), (1, 1)),
        dimension_numbers=("NHWC", "HWIO", "NHWC"),
        preferred_element_type=jnp.float32,
    ).reshape(section_in.shape)
    grad_norm = space_back * silu_slope(normed)
    grad_act = inv_rms * grad_norm - act_f32 * (inv_rms * inv_rms * inv_rms) * jnp.mean(
        grad_norm * act_f32, axis=-1, keepdims=True
    )
    grad_in = (grad_out.astype(jnp.float32) + grad_act).astype(jnp.bfloat16)
    return (cols_space, grad_mid, cols_time, grad_in)


def kernel_term(columns, grads):
    return lax.dot_general(
        flatten_cells(columns),
        flatten_cells(grads),
        (((0,), (0,)), ((), ())),
        preferred_element_type=jnp.float32,
    )


def reduce_over_dp(packed):
    cores = lax.axis_size("core")
    core_idx = lax.axis_index("core")
    by_core = packed.reshape(-1, cores, *packed.shape[1:])
    keep = lax.dynamic_index_in_dim(by_core, core_idx, 1, keepdims=False)
    send = lax.dynamic_index_in_dim(by_core, cores - 1 - core_idx, 1, keepdims=False)
    got = lax.ppermute(send.astype(jnp.bfloat16), "core", [(0, 1), (1, 0)])
    pair_sum = (keep + got.astype(jnp.float32)).astype(jnp.bfloat16)
    gathered = lax.all_to_all(pair_sum, "chip", 0, 0, tiled=True)
    return jnp.sum(gathered.astype(jnp.float32), axis=0)


def local(latents, cotangent, spatial_kernels, temporal_kernels):
    w_spatial = spatial_kernels[0]
    w_temporal = temporal_kernels[0]
    channels = w_spatial.shape[-1]
    w_spatial_flip = w_spatial.reshape(3, 3, -1, channels)[::-1, ::-1].transpose(0, 1, 3, 2)
    micro_count = latents.shape[0]
    section_count = lax.axis_size("section")
    replicas = lax.axis_size("chip") * lax.axis_size("core")
    section_idx = lax.axis_index("section")
    is_first = section_idx == 0
    is_last = section_idx == section_count - 1
    fwd_last = micro_count + section_count - 2
    bwd_first = section_count - 1
    tick_count = micro_count + 2 * section_count - 2
    empty_act = jnp.zeros(latents.shape[1:], jnp.bfloat16)
    stash_in = jnp.zeros((fwd_last + 1,) + latents.shape[1:], jnp.bfloat16)
    stash_mid = jnp.zeros((fwd_last + 1,) + latents.shape[1:], jnp.float32)
    hold_space = jnp.zeros(w_spatial.shape, jnp.float32)
    hold_time = jnp.zeros(w_temporal.shape, jnp.float32)
    recv_act = empty_act
    grad_in = None
    for tick in range(tick_count):
        if grad_in is not None:
            recv_grad = from_behind(grad_in, "section", -1)
        if tick <= fwd_last:
            fresh_in = latents[tick] if tick < micro_count else empty_act
            section_in = jnp.where(is_first, fresh_in, recv_act)
            section_out, middle = section_forward(section_in, w_spatial, w_temporal)
            stash_in = stash_in.at[tick].set(section_in)
            stash_mid = stash_mid.at[tick].set(middle)
            if tick + 1 <= fwd_last:
                recv_act = from_behind(section_out, "section", 1)
        if tick == tick_count - 1:
            hold_space, hold_time = lax.optimization_barrier((hold_space, hold_time))
        if tick >= bwd_first:
            fresh_idx = tick - bwd_first
            fresh_grad = cotangent[fresh_idx] if fresh_idx < micro_count else empty_act
            grad_now = jnp.where(is_last, fresh_grad, recv_grad) if tick > bwd_first else fresh_grad
            micro_idx = tick - 2 * (section_count - 1) + section_idx
            active = (micro_idx >= 0) & (micro_idx < micro_count)
            slot_idx = jnp.clip(micro_idx + section_idx, 0, fwd_last)
            section_in_b = lax.dynamic_index_in_dim(stash_in, slot_idx, 0, keepdims=False)
            middle_b = lax.dynamic_index_in_dim(stash_mid, slot_idx, 0, keepdims=False)
            cols_space, grad_mid, cols_time, grad_in = section_backward(
                grad_now, section_in_b, middle_b, w_spatial_flip, w_temporal
            )
            active_weight = active.astype(jnp.float32)
            hold_space = hold_space + active_weight * kernel_term(cols_space, grad_mid)
            hold_time = hold_time + active_weight * kernel_term(cols_time, grad_now)
            if tick + 1 >= tick_count:
                grad_in = None
    rows_space = w_spatial.shape[0] // replicas
    rows_time = w_temporal.shape[0] // replicas
    packed = jnp.concatenate(
        [
            hold_space.reshape(replicas, rows_space, -1),
            hold_time.reshape(replicas, rows_time, -1),
        ],
        axis=1,
    )
    share = reduce_over_dp(packed)
    share_space, share_time = (share[:rows_space], share[rows_space:])
    cells = (
        micro_count
        * replicas
        * latents.shape[1]
        * latents.shape[2]
        * latents.shape[3]
        * latents.shape[4]
    )
    grad_scale = 1.0 / math.sqrt(cells)
    return ((grad_scale * share_space)[None], (grad_scale * share_time)[None])


def solution(mesh):
    cores = 2
    chip_mesh = Mesh(
        np.asarray(mesh.devices).reshape(mesh.shape["section"], mesh.shape["dp"] // cores, cores),
        ("section", "chip", "core"),
    )
    dp = ("chip", "core")
    in_specs = (
        P(None, dp, None, None, None, None),
        P(None, dp, None, None, None, None),
        P("section", None, None),
        P("section", None, None),
    )
    out_specs = (P("section", dp, None), P("section", dp, None))
    return jax.shard_map(local, mesh=chip_mesh, in_specs=in_specs, out_specs=out_specs, check_vma=False)
```
